512 devices in a mesh: section: 8 (over z), ctx: 8 (over y_hi, x), tp: 8 (over y_lo, core).
Axes of the slice: x: 4, y: 8 (y_hi: 2, y_lo: 4; y = y_hi * 4 + y_lo), z: 8, core: 2. Of those that a mesh axis runs over, the one named last changes fastest.
Arguments:
- block_order: int32 [16], replicated, may hold values from 0 to 15, each once
- plan: int32 [8], replicated, may hold values from 0 to 1
- q_box: bfloat16 [8, 2, 1408, 8192], P('section', None, 'ctx', 'tp'), may hold values from -8 to 8
- k_box: bfloat16 [8, 2, 1408, 1024], P('section', None, ('ctx', 'tp')), may hold values from -8 to 8
- v_box: bfloat16 [8, 2, 1408, 1024], P('section', None, ('ctx', 'tp')), may hold values from -6 to 6
- grad_out: bfloat16 [8, 1408, 8192], P('section', 'ctx', 'tp'), may hold values from -6 to 6
Outputs:
- attn_out: bfloat16 [8, 1408, 8192], P('section', 'ctx', 'tp')
- grad_q: bfloat16 [8, 1408, 8192], P('section', 'ctx', 'tp')
- grad_k: float32 [8, 1408, 1024], P('section', ('ctx', 'tp'))
- grad_v: float32 [8, 1408, 1024], P('section', ('ctx', 'tp'))
The draws below stay inside these ranges and needn't reach their ends.
Inputs may be any that keep to these rules, and one draw needn't show every extreme that they name: `block_order`: a permutation: every block sits in exactly one storage slot, slot j covering storage rows j * 88 to (j + 1) * 88 - 1.
All inputs are finite; a program needn't handle non-finite values.
Results may differ from the reference program's by a relative error of at most 0.012.
Values may be sent and summed in bfloat16 or wider, within the bound.
No kernel may reach another device: no remote copies, remote signals or barrier semaphores. Data moves between devices by JAX's collectives and lax.ppermute only.
A program may use at most 64 MiB of HBM per device.

```python
import jax
import jax.numpy as jnp
from jax import lax

HEADS = 64
KV_HEADS = 8
HEAD_DIM = 128
MB = 2
SECTIONS = 8
L = 1408
BLOCK = 88
NCHUNK = 16
QW = 8192
KW = 1024


def base_values(key, width):
    shape = (SECTIONS, MB, L, width)
    values = jax.random.normal(jax.random.fold_in(key, 13), shape, jnp.float32)
    return jnp.clip(values, -6.0, 6.0)


def draw_q_box(key, part):
    values = base_values(jax.random.fold_in(key, 21), QW)
    return values.astype(jnp.bfloat16)


def draw_k_box(key, part):
    values = base_values(jax.random.fold_in(key, 31), KW)
    return jnp.clip(values, -8.0, 8.0).astype(jnp.bfloat16)


def with_ends(result, stream_key, low, high):
    dims = result.shape
    index_at = [jax.random.randint(jax.random.fold_in(stream_key, axis), (), 0, dims[axis]) for axis in range(len(dims))]
    result = result.at[tuple(index_at)].set(low)
    longest = dims.index(max(dims))
    index_at[longest] = (index_at[longest] + 1) % dims[longest]
    return result.at[tuple(index_at)].set(high)


def block_scale(key, extent, pieces, least, top_value):
    level, own = 1.0, jax.random.fold_in(key, 6)
    for axis_at, blocks in pieces:
        heights = jnp.exp(jax.random.uniform(jax.random.fold_in(own, axis_at), (blocks,), jnp.float32, least / len(pieces), top_value / len(pieces)))
        level = level * jnp.repeat(heights, extent[axis_at] // blocks).reshape([-1 if axis == axis_at else 1 for axis in range(len(extent))])
    return level


def normal_values(stream_key, shape, spread, limit, pieces=(), held_as=jnp.bfloat16):
    entries = jax.random.normal(stream_key, shape, jnp.float32) * spread
    if len(pieces) > 0:
        entries = block_scale(stream_key, shape, pieces, -0.22, 0.18) * entries
    return jnp.clip(entries, min=-limit, max=limit).astype(held_as)


def setup_inputs(seed: int = 0) -> dict:
    streams_of = jax.random.split(jax.random.key(seed), 7)
    block_order = jax.random.permutation(streams_of[0], NCHUNK).astype(jnp.int32)
    plan = with_ends(jax.random.randint(streams_of[1], (SECTIONS,), 0, MB), jax.random.fold_in(streams_of[1], 1), 0, MB - 1).astype(jnp.int32)
    q_box = draw_q_box(jax.random.fold_in(streams_of[6], 71), 0)
    k_box = draw_k_box(jax.random.fold_in(streams_of[6], 71), 0)
    v_box = normal_values(streams_of[4], (SECTIONS, MB, L, KW), 1.0, 6.0, ((0, 8), (2, 64)))
    grad_out = normal_values(streams_of[5], (SECTIONS, L, QW), 1.0, 6.0, ((0, 8), (1, 8), (2, 8)))
    return {"block_order": block_order, "plan": plan, "q_box": q_box, "k_box": k_box, "v_box": v_box, "grad_out": grad_out}


NEG = -1e30


def head_grads(q_head, k_head, v_head, do_head, visible):
    scale = HEAD_DIM ** -0.5
    scores = jnp.dot(q_head, k_head.T, preferred_element_type=jnp.float32) * scale
    scores = jnp.where(visible, scores, NEG)
    top_score = jnp.max(scores, axis=1, keepdims=True)
    totals = jnp.sum(jnp.where(visible, jnp.exp(scores - top_score), 0.0), axis=1, keepdims=True)
    log_total = top_score + jnp.log(totals)
    probs = jnp.where(visible, jnp.exp(scores - log_total), 0.0)
    probs_low = probs.astype(jnp.bfloat16)
    attended = jnp.dot(probs_low, v_head, preferred_element_type=jnp.float32)
    delta = jnp.sum(do_head.astype(jnp.float32) * attended, axis=1, keepdims=True)
    dprobs = jnp.dot(do_head, v_head.T, preferred_element_type=jnp.float32)
    dscores = (probs * (dprobs - delta)).astype(jnp.bfloat16)
    q_grad = (jnp.dot(dscores, k_head, preferred_element_type=jnp.float32) * scale).astype(jnp.bfloat16)
    k_grad = jnp.dot(dscores.T, q_head, preferred_element_type=jnp.float32) * scale
    v_grad = jnp.dot(probs_low.T, do_head, preferred_element_type=jnp.float32)
    return attended.astype(jnp.bfloat16), q_grad, k_grad, v_grad


def reference(block_order, plan, q_box, k_box, v_box, grad_out):
    positions = (block_order[:, None] * BLOCK + jnp.arange(BLOCK, dtype=jnp.int32)[None, :]).reshape(L)
    visible = positions[None, :] <= positions[:, None]
    group = HEADS // KV_HEADS
    outputs = []
    grads_q = []
    grads_k = []
    grads_v = []
    for section in range(SECTIONS):
        source = (section - 1) % SECTIONS
        target = (section + 1) % SECTIONS
        picked = plan[section]
        q_all = lax.dynamic_index_in_dim(q_box[source], picked, 0, keepdims=False)
        k_all = lax.dynamic_index_in_dim(k_box[source], picked, 0, keepdims=False)
        v_all = lax.dynamic_index_in_dim(v_box[source], picked, 0, keepdims=False)
        do_all = grad_out[target]
        q_heads = q_all.reshape(L, HEADS, HEAD_DIM).transpose(1, 0, 2)
        do_heads = do_all.reshape(L, HEADS, HEAD_DIM).transpose(1, 0, 2)
        k_heads = k_all.reshape(L, KV_HEADS, HEAD_DIM).transpose(1, 0, 2)
        v_heads = v_all.reshape(L, KV_HEADS, HEAD_DIM).transpose(1, 0, 2)

        def one_head(head_index):
            kv_index = head_index // group
            q_head = lax.dynamic_index_in_dim(q_heads, head_index, 0, keepdims=False)
            do_head = lax.dynamic_index_in_dim(do_heads, head_index, 0, keepdims=False)
            k_head = lax.dynamic_index_in_dim(k_heads, kv_index, 0, keepdims=False)
            v_head = lax.dynamic_index_in_dim(v_heads, kv_index, 0, keepdims=False)
            return head_grads(q_head, k_head, v_head, do_head, visible)

        attended, q_grad, k_grad, v_grad = lax.map(one_head, jnp.arange(HEADS, dtype=jnp.int32))
        outputs.append(attended.transpose(1, 0, 2).reshape(L, QW))
        grads_q.append(q_grad.transpose(1, 0, 2).reshape(L, QW))
        k_sum = jnp.sum(k_grad.reshape(KV_HEADS, group, L, HEAD_DIM), axis=1)
        v_sum = jnp.sum(v_grad.reshape(KV_HEADS, group, L, HEAD_DIM), axis=1)
        grads_k.append(k_sum.transpose(1, 0, 2).reshape(L, KW))
        grads_v.append(v_sum.transpose(1, 0, 2).reshape(L, KW))
    return (jnp.stack(outputs), jnp.stack(grads_q), jnp.stack(grads_k), jnp.stack(grads_v))
```

```python
import jax
import jax.numpy as jnp
from jax import lax
from jax.sharding import PartitionSpec as P

HEAD_DIM = 128


NEG = -1e30


def passed_along(block, axis, distance):
    devices = range(lax.axis_size(axis))
    route = [((i - distance) % len(devices), i) for i in devices]
    return lax.ppermute(block, axis, route)


def body(block_order, plan, q_box, k_box, v_box, grad_out):
    tp_count = lax.axis_size("tp")
    ctx_count = lax.axis_size("ctx")
    section_count = lax.axis_size("section")
    tok_rows = q_box.shape[2]
    kv_rows = k_box.shape[2]
    seq_rows = tok_rows * ctx_count
    block_len = seq_rows // block_order.shape[0]
    head_size = HEAD_DIM
    heads_local = q_box.shape[3] // head_size
    kv_local = k_box.shape[3] // head_size // tp_count
    group = heads_local // kv_local
    kv_width = kv_local * head_size
    scale = head_size ** (-0.5)
    section_rank = lax.axis_index("section")

    receiver = (section_rank + 1) % section_count
    wanted = lax.dynamic_index_in_dim(plan, receiver, 0, keepdims=False)
    q_send = lax.dynamic_index_in_dim(q_box[0], wanted, 0, keepdims=False)
    k_send = lax.dynamic_index_in_dim(k_box[0], wanted, 0, keepdims=False)
    v_send = lax.dynamic_index_in_dim(v_box[0], wanted, 0, keepdims=False)
    kv_send = jnp.stack(
        [k_send.reshape(kv_rows, -1, head_size), v_send.reshape(kv_rows, -1, head_size)], axis=2
    ).reshape(kv_rows, -1)
    queries, kv_rows_in = passed_along((q_send, kv_send), "section", 1)
    cotangent = passed_along(grad_out[0], "section", -1)

    kv_tok = lax.all_to_all(kv_rows_in, "tp", split_axis=1, concat_axis=0, tiled=True)
    kv_full = lax.all_gather(kv_tok, "ctx", axis=0, tiled=True)
    kv_full = kv_full.reshape(seq_rows, kv_local, 2, head_size)
    key_heads = kv_full[:, :, 0, :]
    value_heads = kv_full[:, :, 1, :]

    positions = (
        block_order[:, None] * block_len + jnp.arange(block_len, dtype=jnp.int32)[None, :]
    ).reshape(seq_rows)
    query_pos = lax.dynamic_slice_in_dim(positions, lax.axis_index("ctx") * tok_rows, tok_rows)
    visible = (positions[None, :] <= query_pos[:, None])[None, None]

    q4 = queries.reshape(tok_rows, kv_local, group, head_size)
    do4 = cotangent.reshape(tok_rows, kv_local, group, head_size)
    scores = jnp.einsum("qgjd,kgd->gjqk", q4, key_heads, preferred_element_type=jnp.float32) * scale
    scores = jnp.where(visible, scores, NEG)
    top_score = jnp.max(scores, axis=-1, keepdims=True)
    totals = jnp.sum(jnp.where(visible, jnp.exp(scores - top_score), 0.0), axis=-1, keepdims=True)
    log_total = top_score + jnp.log(totals)
    probs = jnp.where(visible, jnp.exp(scores - log_total), 0.0)
    probs_low = probs.astype(jnp.bfloat16)
    attended = jnp.einsum(
        "gjqk,kgd->qgjd", probs_low, value_heads, preferred_element_type=jnp.float32
    )
    delta = jnp.sum(do4.astype(jnp.float32) * attended, axis=-1)
    dprobs = jnp.einsum("qgjd,kgd->gjqk", do4, value_heads, preferred_element_type=jnp.float32)
    dscores = (probs * (dprobs - jnp.transpose(delta, (1, 2, 0))[..., None])).astype(jnp.bfloat16)
    q_grad = (
        jnp.einsum("gjqk,kgd->qgjd", dscores, key_heads, preferred_element_type=jnp.float32) * scale
    ).astype(jnp.bfloat16)
    key_grad = jnp.einsum("gjqk,qgjd->kgd", dscores, q4, preferred_element_type=jnp.float32) * scale
    value_grad = jnp.einsum("gjqk,qgjd->kgd", probs_low, do4, preferred_element_type=jnp.float32)

    attended_flat = attended.astype(jnp.bfloat16).reshape(tok_rows, heads_local * head_size)
    q_grad_flat = q_grad.reshape(tok_rows, heads_local * head_size)
    grad_terms = jnp.stack([key_grad, value_grad], axis=2).reshape(seq_rows, 2 * kv_width)
    own_grads = lax.psum_scatter(grad_terms, "ctx", scatter_dimension=0, tiled=True)
    tok_grads = lax.all_to_all(own_grads, "tp", split_axis=0, concat_axis=1, tiled=True)
    tok_grads = tok_grads.reshape(kv_rows, -1, 2, head_size)
    k_grad_tokens = tok_grads[:, :, 0, :].reshape(kv_rows, -1)
    v_grad_tokens = tok_grads[:, :, 1, :].reshape(kv_rows, -1)
    return (attended_flat[None], q_grad_flat[None], k_grad_tokens[None], v_grad_tokens[None])


def solution(mesh):
    in_specs = (
        P(),
        P(),
        P("section", None, "ctx", "tp"),
        P("section", None, ("ctx", "tp"), None),
        P("section", None, ("ctx", "tp"), None),
        P("section", "ctx", "tp"),
    )
    out_specs = (
        P("section", "ctx", "tp"),
        P("section", "ctx", "tp"),
        P("section", ("ctx", "tp"), None),
        P("section", ("ctx", "tp"), None),
    )
    return jax.shard_map(body, mesh=mesh, in_specs=in_specs, out_specs=out_specs, check_vma=False)
```

```python
import jax
import jax.numpy as jnp
from jax import lax
from jax.sharding import PartitionSpec as P

HEAD_DIM = 128
CTX_INNER = 4


NEG = -1e30


def passed_along(block, axis, distance):
    devices = range(lax.axis_size(axis))
    route = [((i - distance) % len(devices), i) for i in devices]
    return lax.ppermute(block, axis, route)


def body(block_order, plan, q_box, k_box, v_box, grad_out):
    tp_count = lax.axis_size("tp")
    ctx_count = lax.axis_size("ctx")
    section_count = lax.axis_size("section")
    tok_rows = q_box.shape[2]
    kv_rows = k_box.shape[2]
    seq_rows = tok_rows * ctx_count
    block_len = seq_rows // block_order.shape[0]
    head_size = HEAD_DIM
    heads_local = q_box.shape[3] // head_size
    kv_local = k_box.shape[3] // head_size // tp_count
    group = heads_local // kv_local
    kv_width = kv_local * head_size
    scale = head_size ** (-0.5)
    section_rank = lax.axis_index("section")

    receiver = (section_rank + 1) % section_count
    wanted = lax.dynamic_index_in_dim(plan, receiver, 0, keepdims=False)
    q_send = lax.dynamic_index_in_dim(q_box[0], wanted, 0, keepdims=False)
    k_send = lax.dynamic_index_in_dim(k_box[0], wanted, 0, keepdims=False)
    v_send = lax.dynamic_index_in_dim(v_box[0], wanted, 0, keepdims=False)
    kv_send = jnp.stack(
        [k_send.reshape(kv_rows, -1, head_size), v_send.reshape(kv_rows, -1, head_size)], axis=2
    ).reshape(kv_rows, -1)
    queries, kv_rows_in = passed_along((q_send, kv_send), "section", 1)
    cotangent = passed_along(grad_out[0], "section", -1)

    kv_tok = lax.all_to_all(kv_rows_in, "tp", split_axis=1, concat_axis=0, tiled=True)
    inner_count = CTX_INNER
    outer_count = ctx_count // inner_count
    ctx_rank = lax.axis_index("ctx")
    inner_rank = ctx_rank % inner_count
    outer_rank = ctx_rank // inner_count
    swap = [(c, (c + inner_count) % ctx_count) for c in range(ctx_count)]

    def inner_shift(k):
        return [
            (o * inner_count + i, o * inner_count + (i + k) % inner_count)
            for o in range(outer_count)
            for i in range(inner_count)
        ]

    partner = lax.ppermute(kv_tok, "ctx", swap)
    pair = jnp.stack([kv_tok, partner])
    arrived_kv = [pair] + [lax.ppermute(pair, "ctx", inner_shift(k)) for k in range(1, inner_count)]
    kv_full = jnp.stack(arrived_kv).reshape(seq_rows, kv_local, 2, head_size)
    key_heads = kv_full[:, :, 0, :]
    value_heads = kv_full[:, :, 1, :]

    positions = (
        block_order[:, None] * block_len + jnp.arange(block_len, dtype=jnp.int32)[None, :]
    ).reshape(ctx_count, tok_rows)
    shift_ids = jnp.arange(inner_count, dtype=jnp.int32)[:, None]
    side_ids = jnp.arange(outer_count, dtype=jnp.int32)[None, :]
    key_ctx = ((outer_rank + side_ids) % outer_count) * inner_count + (
        (inner_rank - shift_ids) % inner_count
    )
    key_pos = jnp.take(positions, key_ctx.reshape(-1), axis=0).reshape(seq_rows)
    query_pos = lax.dynamic_index_in_dim(positions, ctx_rank, 0, keepdims=False)
    visible = (key_pos[None, :] <= query_pos[:, None])[None, None]

    q4 = queries.reshape(tok_rows, kv_local, group, head_size)
    do4 = cotangent.reshape(tok_rows, kv_local, group, head_size)
    scores = jnp.einsum("qgjd,kgd->gjqk", q4, key_heads, preferred_element_type=jnp.float32) * scale
    scores = jnp.where(visible, scores, NEG)
    top_score = jnp.max(scores, axis=-1, keepdims=True)
    totals = jnp.sum(jnp.where(visible, jnp.exp(scores - top_score), 0.0), axis=-1, keepdims=True)
    log_total = top_score + jnp.log(totals)
    probs = jnp.where(visible, jnp.exp(scores - log_total), 0.0)
    probs_low = probs.astype(jnp.bfloat16)
    attended = jnp.einsum(
        "gjqk,kgd->qgjd", probs_low, value_heads, preferred_element_type=jnp.float32
    )
    delta = jnp.sum(do4.astype(jnp.float32) * attended, axis=-1)
    dprobs = jnp.einsum("qgjd,kgd->gjqk", do4, value_heads, preferred_element_type=jnp.float32)
    dscores = (probs * (dprobs - jnp.transpose(delta, (1, 2, 0))[..., None])).astype(jnp.bfloat16)
    q_grad = (
        jnp.einsum("gjqk,kgd->qgjd", dscores, key_heads, preferred_element_type=jnp.float32) * scale
    ).astype(jnp.bfloat16)
    key_grad = jnp.einsum("gjqk,qgjd->kgd", dscores, q4, preferred_element_type=jnp.float32) * scale
    value_grad = jnp.einsum("gjqk,qgjd->kgd", probs_low, do4, preferred_element_type=jnp.float32)

    attended_flat = attended.astype(jnp.bfloat16).reshape(tok_rows, heads_local * head_size)
    q_grad_flat = q_grad.reshape(tok_rows, heads_local * head_size)
    grad_terms = jnp.stack([key_grad, value_grad], axis=2).reshape(
        inner_count, outer_count, tok_rows, 2 * kv_width
    )
    gathered = grad_terms[0]
    for k in range(1, inner_count):
        gathered = gathered + lax.ppermute(grad_terms[(-k) % inner_count], "ctx", inner_shift(k))
    own_grads = gathered[0] + lax.ppermute(gathered[1], "ctx", swap)
    tok_grads = lax.all_to_all(own_grads, "tp", split_axis=0, concat_axis=1, tiled=True)
    tok_grads = tok_grads.reshape(kv_rows, -1, 2, head_size)
    k_grad_tokens = tok_grads[:, :, 0, :].reshape(kv_rows, -1)
    v_grad_tokens = tok_grads[:, :, 1, :].reshape(kv_rows, -1)
    return (attended_flat[None], q_grad_flat[None], k_grad_tokens[None], v_grad_tokens[None])


def solution(mesh):
    in_specs = (
        P(),
        P(),
        P("section", None, "ctx", "tp"),
        P("section", None, ("ctx", "tp"), None),
        P("section", None, ("ctx", "tp"), None),
        P("section", "ctx", "tp"),
    )
    out_specs = (
        P("section", "ctx", "tp"),
        P("section", "ctx", "tp"),
        P("section", ("ctx", "tp"), None),
        P("section", ("ctx", "tp"), None),
    )
    return jax.shard_map(body, mesh=mesh, in_specs=in_specs, out_specs=out_specs, check_vma=False)
```

```python
import jax
import jax.numpy as jnp
from jax import lax
from jax.sharding import PartitionSpec as P

HEAD_DIM = 128


NEG = -1e30


def passed_along(block, axis, distance):
    devices = range(lax.axis_size(axis))
    route = [((i - distance) % len(devices), i) for i in devices]
    return lax.ppermute(block, axis, route)


def body(block_order, plan, q_box, k_box, v_box, grad_out):
    tp_count = lax.axis_size("tp")
    ctx_count = lax.axis_size("ctx")
    section_count = lax.axis_size("section")
    tok_rows = q_box.shape[2]
    kv_rows = k_box.shape[2]
    seq_rows = tok_rows * ctx_count
    block_len = seq_rows // block_order.shape[0]
    head_size = HEAD_DIM
    heads_local = q_box.shape[3] // head_size
    kv_local = k_box.shape[3] // head_size // tp_count
    group = heads_local // kv_local
    kv_width = kv_local * head_size
    scale = head_size ** (-0.5)
    section_rank = lax.axis_index("section")

    receiver = (section_rank + 1) % section_count
    wanted = lax.dynamic_index_in_dim(plan, receiver, 0, keepdims=False)
    q_send = lax.dynamic_index_in_dim(q_box[0], wanted, 0, keepdims=False)
    k_send = lax.dynamic_index_in_dim(k_box[0], wanted, 0, keepdims=False)
    v_send = lax.dynamic_index_in_dim(v_box[0], wanted, 0, keepdims=False)
    kv_send = jnp.stack(
        [k_send.reshape(kv_rows, -1, head_size), v_send.reshape(kv_rows, -1, head_size)], axis=2
    ).reshape(kv_rows, -1)
    queries, kv_rows_in = passed_along((q_send, kv_send), "section", 1)
    cotangent = passed_along(grad_out[0], "section", -1)

    plane = ("ctx", "tp")
    kv_pieces = kv_rows_in.reshape(1, kv_rows, tp_count, 2 * kv_width).transpose(0, 2, 1, 3)
    kv_pieces = jnp.broadcast_to(kv_pieces, (ctx_count, tp_count, kv_rows, 2 * kv_width))
    kv_pieces = kv_pieces.reshape(ctx_count * tp_count * kv_rows, 2 * kv_width)
    kv_full = lax.all_to_all(kv_pieces, plane, split_axis=0, concat_axis=0, tiled=True)
    kv_full = kv_full.reshape(seq_rows, kv_local, 2, head_size)
    key_heads = kv_full[:, :, 0, :]
    value_heads = kv_full[:, :, 1, :]
    ctx_rank = lax.axis_index("ctx")

    positions = (
        block_order[:, None] * block_len + jnp.arange(block_len, dtype=jnp.int32)[None, :]
    ).reshape(ctx_count, tok_rows)
    key_pos = positions.reshape(seq_rows)
    query_pos = lax.dynamic_index_in_dim(positions, ctx_rank, 0, keepdims=False)
    visible = (key_pos[None, :] <= query_pos[:, None])[None, None]

    q4 = queries.reshape(tok_rows, kv_local, group, head_size)
    do4 = cotangent.reshape(tok_rows, kv_local, group, head_size)
    scores = jnp.einsum("qgjd,kgd->gjqk", q4, key_heads, preferred_element_type=jnp.float32) * scale
    scores = jnp.where(visible, scores, NEG)
    top_score = jnp.max(scores, axis=-1, keepdims=True)
    totals = jnp.sum(jnp.where(visible, jnp.exp(scores - top_score), 0.0), axis=-1, keepdims=True)
    log_total = top_score + jnp.log(totals)
    probs = jnp.where(visible, jnp.exp(scores - log_total), 0.0)
    probs_low = probs.astype(jnp.bfloat16)
    attended = jnp.einsum(
        "gjqk,kgd->qgjd", probs_low, value_heads, preferred_element_type=jnp.float32
    )
    delta = jnp.sum(do4.astype(jnp.float32) * attended, axis=-1)
    dprobs = jnp.einsum("qgjd,kgd->gjqk", do4, value_heads, preferred_element_type=jnp.float32)
    dscores = (probs * (dprobs - jnp.transpose(delta, (1, 2, 0))[..., None])).astype(jnp.bfloat16)
    q_grad = (
        jnp.einsum("gjqk,kgd->qgjd", dscores, key_heads, preferred_element_type=jnp.float32) * scale
    ).astype(jnp.bfloat16)
    key_grad = jnp.einsum("gjqk,qgjd->kgd", dscores, q4, preferred_element_type=jnp.float32) * scale
    value_grad = jnp.einsum("gjqk,qgjd->kgd", probs_low, do4, preferred_element_type=jnp.float32)

    attended_flat = attended.astype(jnp.bfloat16).reshape(tok_rows, heads_local * head_size)
    q_grad_flat = q_grad.reshape(tok_rows, heads_local * head_size)
    grad_terms = jnp.stack([key_grad, value_grad], axis=2).reshape(seq_rows, 2 * kv_width)
    grad_parts = lax.all_to_all(grad_terms, plane, split_axis=0, concat_axis=0, tiled=True)
    grad_parts = grad_parts.reshape(ctx_count, tp_count, kv_rows, kv_local, 2, head_size)
    own_grads = jnp.sum(grad_parts, axis=0)
    k_grad_tokens = own_grads[:, :, :, 0, :].transpose(1, 0, 2, 3).reshape(kv_rows, -1)
    v_grad_tokens = own_grads[:, :, :, 1, :].transpose(1, 0, 2, 3).reshape(kv_rows, -1)
    return (attended_flat[None], q_grad_flat[None], k_grad_tokens[None], v_grad_tokens[None])


def solution(mesh):
    in_specs = (
        P(),
        P(),
        P("section", None, "ctx", "tp"),
        P("section", None, ("ctx", "tp"), None),
        P("section", None, ("ctx", "tp"), None),
        P("section", "ctx", "tp"),
    )
    out_specs = (
        P("section", "ctx", "tp"),
        P("section", "ctx", "tp"),
        P("section", ("ctx", "tp"), None),
        P("section", ("ctx", "tp"), None),
    )
    return jax.shard_map(body, mesh=mesh, in_specs=in_specs, out_specs=out_specs, check_vma=False)
```

```python
import jax
import jax.numpy as jnp
from jax import lax
from jax.sharding import PartitionSpec as P

HEAD_DIM = 128


NEG = -1e30


def passed_along(block, axis, distance):
    devices = range(lax.axis_size(axis))
    route = [((i - distance) % len(devices), i) for i in devices]
    return lax.ppermute(block, axis, route)


def body(block_order, plan, q_box, k_box, v_box, grad_out):
    tp_count = lax.axis_size("tp")
    ctx_count = lax.axis_size("ctx")
    section_count = lax.axis_size("section")
    tok_rows = q_box.shape[2]
    kv_rows = k_box.shape[2]
    seq_rows = tok_rows * ctx_count
    block_len = seq_rows // block_order.shape[0]
    head_size = HEAD_DIM
    heads_local = q_box.shape[3] // head_size
    kv_local = k_box.shape[3] // head_size // tp_count
    group = heads_local // kv_local
    kv_width = kv_local * head_size
    scale = head_size ** (-0.5)
    section_rank = lax.axis_index("section")

    receiver = (section_rank + 1) % section_count
    wanted = lax.dynamic_index_in_dim(plan, receiver, 0, keepdims=False)
    q_send = lax.dynamic_index_in_dim(q_box[0], wanted, 0, keepdims=False)
    k_send = lax.dynamic_index_in_dim(k_box[0], wanted, 0, keepdims=False)
    v_send = lax.dynamic_index_in_dim(v_box[0], wanted, 0, keepdims=False)
    kv_send = jnp.stack(
        [k_send.reshape(kv_rows, -1, head_size), v_send.reshape(kv_rows, -1, head_size)], axis=2
    ).reshape(kv_rows, -1)
    queries, kv_rows_in = passed_along((q_send, kv_send), "section", 1)
    cotangent = passed_along(grad_out[0], "section", -1)

    plane = ("ctx", "tp")
    kv_pieces = kv_rows_in.reshape(1, kv_rows, tp_count, 2 * kv_width).transpose(0, 2, 1, 3)
    kv_pieces = jnp.broadcast_to(kv_pieces, (ctx_count, tp_count, kv_rows, 2 * kv_width))
    kv_pieces = kv_pieces.reshape(ctx_count * tp_count * kv_rows, 2 * kv_width)
    kv_full = lax.all_to_all(kv_pieces, plane, split_axis=0, concat_axis=0, tiled=True)
    kv_full = kv_full.reshape(seq_rows, kv_local, 2, head_size)
    key_heads = kv_full[:, :, 0, :]
    value_heads = kv_full[:, :, 1, :]
    ctx_rank = lax.axis_index("ctx")

    positions = (
        block_order[:, None] * block_len + jnp.arange(block_len, dtype=jnp.int32)[None, :]
    ).reshape(ctx_count, tok_rows)
    key_pos = positions.reshape(seq_rows)
    query_pos = lax.dynamic_index_in_dim(positions, ctx_rank, 0, keepdims=False)
    visible = (key_pos[None, :] <= query_pos[:, None])[None, None]

    q4 = queries.reshape(tok_rows, kv_local, group, head_size)
    do4 = cotangent.reshape(tok_rows, kv_local, group, head_size)
    scores = jnp.einsum("qgjd,kgd->gjqk", q4, key_heads, preferred_element_type=jnp.float32) * scale
    scores = jnp.where(visible, scores, NEG)
    top_score = jnp.max(scores, axis=-1, keepdims=True)
    totals = jnp.sum(jnp.where(visible, jnp.exp(scores - top_score), 0.0), axis=-1, keepdims=True)
    log_total = top_score + jnp.log(totals)
    probs = jnp.where(visible, jnp.exp(scores - log_total), 0.0)
    probs_low = probs.astype(jnp.bfloat16)
    attended = jnp.einsum(
        "gjqk,kgd->qgjd", probs_low, value_heads, preferred_element_type=jnp.float32
    )
    delta = jnp.sum(do4.astype(jnp.float32) * attended, axis=-1)
    dprobs = jnp.einsum("qgjd,kgd->gjqk", do4, value_heads, preferred_element_type=jnp.float32)
    dscores = (probs * (dprobs - jnp.transpose(delta, (1, 2, 0))[..., None])).astype(jnp.bfloat16)
    q_grad = (
        jnp.einsum("gjqk,kgd->qgjd", dscores, key_heads, preferred_element_type=jnp.float32) * scale
    ).astype(jnp.bfloat16)
    key_grad = jnp.einsum("gjqk,qgjd->kgd", dscores, q4, preferred_element_type=jnp.float32) * scale
    value_grad = jnp.einsum("gjqk,qgjd->kgd", probs_low, do4, preferred_element_type=jnp.float32)

    attended_flat = attended.astype(jnp.bfloat16).reshape(tok_rows, heads_local * head_size)
    q_grad_flat = q_grad.reshape(tok_rows, heads_local * head_size)
    def to_owners(term):
        sent = term.reshape(seq_rows, kv_width).astype(jnp.bfloat16)
        parts = lax.all_to_all(sent, plane, split_axis=0, concat_axis=0, tiled=True)
        parts = parts.reshape(ctx_count, tp_count, kv_rows, kv_width).astype(jnp.float32)
        return jnp.sum(parts, axis=0).transpose(1, 0, 2).reshape(kv_rows, -1)

    v_grad_tokens = to_owners(value_grad)
    k_grad_tokens = to_owners(key_grad)
    return (attended_flat[None], q_grad_flat[None], k_grad_tokens[None], v_grad_tokens[None])


def solution(mesh):
    in_specs = (
        P(),
        P(),
        P("section", None, "ctx", "tp"),
        P("section", None, ("ctx", "tp"), None),
        P("section", None, ("ctx", "tp"), None),
        P("section", "ctx", "tp"),
    )
    out_specs = (
        P("section", "ctx", "tp"),
        P("section", "ctx", "tp"),
        P("section", ("ctx", "tp"), None),
        P("section", ("ctx", "tp"), None),
    )
    return jax.shard_map(body, mesh=mesh, in_specs=in_specs, out_specs=out_specs, check_vma=False)
```

```python
import jax
import jax.numpy as jnp
from jax import lax
from jax.sharding import PartitionSpec as P

HEAD_DIM = 128


NEG = -1e30


def passed_along(block, axis, distance):
    devices = range(lax.axis_size(axis))
    route = [((i - distance) % len(devices), i) for i in devices]
    return lax.ppermute(block, axis, route)


def body(block_order, plan, q_box, k_box, v_box, grad_out):
    tp_count = lax.axis_size("tp")
    ctx_count = lax.axis_size("ctx")
    section_count = lax.axis_size("section")
    tok_rows = q_box.shape[2]
    kv_rows = k_box.shape[2]
    seq_rows = tok_rows * ctx_count
    block_len = seq_rows // block_order.shape[0]
    head_size = HEAD_DIM
    heads_local = q_box.shape[3] // head_size
    kv_local = k_box.shape[3] // head_size // tp_count
    group = heads_local // kv_local
    kv_width = kv_local * head_size
    scale = head_size ** (-0.5)
    section_rank = lax.axis_index("section")

    receiver = (section_rank + 1) % section_count
    wanted = lax.dynamic_index_in_dim(plan, receiver, 0, keepdims=False)
    q_send = lax.dynamic_index_in_dim(q_box[0], wanted, 0, keepdims=False)
    k_send = lax.dynamic_index_in_dim(k_box[0], wanted, 0, keepdims=False)
    v_send = lax.dynamic_index_in_dim(v_box[0], wanted, 0, keepdims=False)
    kv_send = jnp.stack(
        [k_send.reshape(kv_rows, -1, head_size), v_send.reshape(kv_rows, -1, head_size)], axis=2
    ).reshape(kv_rows, -1)
    queries, kv_rows_in = passed_along((q_send, kv_send), "section", 1)
    cotangent = passed_along(grad_out[0], "section", -1)

    plane = ("ctx", "tp")
    kv_pieces = kv_rows_in.reshape(1, kv_rows, tp_count, 2 * kv_width).transpose(0, 2, 1, 3)
    kv_pieces = jnp.broadcast_to(kv_pieces, (ctx_count, tp_count, kv_rows, 2 * kv_width))
    kv_pieces = kv_pieces.reshape(ctx_count * tp_count * kv_rows, 2 * kv_width)
    kv_full = lax.all_to_all(kv_pieces, plane, split_axis=0, concat_axis=0, tiled=True)
    kv_full = kv_full.reshape(seq_rows, kv_local, 2, head_size)
    key_heads = kv_full[:, :, 0, :]
    value_heads = kv_full[:, :, 1, :]
    ctx_rank = lax.axis_index("ctx")

    positions = (
        block_order[:, None] * block_len + jnp.arange(block_len, dtype=jnp.int32)[None, :]
    ).reshape(ctx_count, tok_rows)
    key_pos = positions.reshape(seq_rows)
    query_pos = lax.dynamic_index_in_dim(positions, ctx_rank, 0, keepdims=False)
    visible = (key_pos[None, :] <= query_pos[:, None])[None, None]

    q4 = queries.reshape(tok_rows, kv_local, group, head_size)
    do4 = cotangent.reshape(tok_rows, kv_local, group, head_size)
    scores = jnp.einsum("qgjd,kgd->gjqk", q4, key_heads, preferred_element_type=jnp.float32) * scale
    scores = jnp.where(visible, scores, NEG)
    top_score = jnp.max(scores, axis=-1, keepdims=True)
    totals = jnp.sum(jnp.where(visible, jnp.exp(scores - top_score), 0.0), axis=-1, keepdims=True)
    log_total = top_score + jnp.log(totals)
    probs = jnp.where(visible, jnp.exp(scores - log_total), 0.0)
    probs_low = probs.astype(jnp.bfloat16)
    attended = jnp.einsum(
        "gjqk,kgd->qgjd", probs_low, value_heads, preferred_element_type=jnp.float32
    )
    delta = jnp.sum(do4.astype(jnp.float32) * attended, axis=-1)
    dprobs = jnp.einsum("qgjd,kgd->gjqk", do4, value_heads, preferred_element_type=jnp.float32)
    dscores = (probs * (dprobs - jnp.transpose(delta, (1, 2, 0))[..., None])).astype(jnp.bfloat16)
    q_grad = (
        jnp.einsum("gjqk,kgd->qgjd", dscores, key_heads, preferred_element_type=jnp.float32) * scale
    ).astype(jnp.bfloat16)
    key_grad = jnp.einsum("gjqk,qgjd->kgd", dscores, q4, preferred_element_type=jnp.float32) * scale
    value_grad = jnp.einsum("gjqk,qgjd->kgd", probs_low, do4, preferred_element_type=jnp.float32)

    attended_flat = attended.astype(jnp.bfloat16).reshape(tok_rows, heads_local * head_size)
    q_grad_flat = q_grad.reshape(tok_rows, heads_local * head_size)
    grad_terms = jnp.stack([key_grad, value_grad], axis=2).reshape(seq_rows, 2 * kv_width)
    grad_parts = lax.all_to_all(
        grad_terms.astype(jnp.bfloat16), plane, split_axis=0, concat_axis=0, tiled=True
    )
    grad_parts = grad_parts.reshape(ctx_count, tp_count, kv_rows, kv_local, 2, head_size)
    own_grads = jnp.sum(grad_parts.astype(jnp.float32), axis=0)
    k_grad_tokens = own_grads[:, :, :, 0, :].transpose(1, 0, 2, 3).reshape(kv_rows, -1)
    v_grad_tokens = own_grads[:, :, :, 1, :].transpose(1, 0, 2, 3).reshape(kv_rows, -1)
    return (attended_flat[None], q_grad_flat[None], k_grad_tokens[None], v_grad_tokens[None])


def solution(mesh):
    in_specs = (
        P(),
        P(),
        P("section", None, "ctx", "tp"),
        P("section", None, ("ctx", "tp"), None),
        P("section", None, ("ctx", "tp"), None),
        P("section", "ctx", "tp"),
    )
    out_specs = (
        P("section", "ctx", "tp"),
        P("section", "ctx", "tp"),
        P("section", ("ctx", "tp"), None),
        P("section", ("ctx", "tp"), None),
    )
    return jax.shard_map(body, mesh=mesh, in_specs=in_specs, out_specs=out_specs, check_vma=False)
```

```python
import jax
import jax.numpy as jnp
from jax import lax
from jax.sharding import PartitionSpec as P

HEAD_DIM = 128


NEG = -1e30


def passed_along(block, axis, distance):
    devices = range(lax.axis_size(axis))
    route = [((i - distance) % len(devices), i) for i in devices]
    return lax.ppermute(block, axis, route)


def plane_step(block_order, plan, q_box, k_box, v_box, grad_out):
    tp_count = lax.axis_size("tp")
    ctx_count = lax.axis_size("ctx")
    section_count = lax.axis_size("section")
    tok_rows = q_box.shape[2]
    kv_rows = k_box.shape[2]
    seq_rows = tok_rows * ctx_count
    block_len = seq_rows // block_order.shape[0]
    head_size = HEAD_DIM
    heads_local = q_box.shape[3] // head_size
    kv_local = k_box.shape[3] // head_size // tp_count
    group = heads_local // kv_local
    kv_width = kv_local * head_size
    scale = head_size ** (-0.5)
    section_rank = lax.axis_index("section")

    receiver = (section_rank + 1) % section_count
    wanted = lax.dynamic_index_in_dim(plan, receiver, 0, keepdims=False)
    q_send = lax.dynamic_index_in_dim(q_box[0], wanted, 0, keepdims=False)
    k_send = lax.dynamic_index_in_dim(k_box[0], wanted, 0, keepdims=False)
    v_send = lax.dynamic_index_in_dim(v_box[0], wanted, 0, keepdims=False)
    kv_send = jnp.stack(
        [k_send.reshape(kv_rows, -1, head_size), v_send.reshape(kv_rows, -1, head_size)], axis=2
    ).reshape(kv_rows, -1)
    kv_rows_in = passed_along(kv_send, "section", 1)
    queries = passed_along(q_send, "section", 1)

    plane = ("ctx", "tp")
    kv_pieces = kv_rows_in.reshape(1, kv_rows, tp_count, 2 * kv_width).transpose(0, 2, 1, 3)
    kv_pieces = jnp.broadcast_to(kv_pieces, (ctx_count, tp_count, kv_rows, 2 * kv_width))
    kv_pieces = kv_pieces.reshape(ctx_count * tp_count * kv_rows, 2 * kv_width)
    kv_pieces, do_send = lax.optimization_barrier((kv_pieces, grad_out[0]))
    kv_full = lax.all_to_all(kv_pieces, plane, split_axis=0, concat_axis=0, tiled=True)
    cotangent = passed_along(do_send, "section", -1)
    kv_full = kv_full.reshape(seq_rows, kv_local, 2, head_size)
    key_heads = kv_full[:, :, 0, :]
    value_heads = kv_full[:, :, 1, :]
    ctx_rank = lax.axis_index("ctx")

    positions = (
        block_order[:, None] * block_len + jnp.arange(block_len, dtype=jnp.int32)[None, :]
    ).reshape(ctx_count, tok_rows)
    key_pos = positions.reshape(seq_rows)
    query_pos = lax.dynamic_index_in_dim(positions, ctx_rank, 0, keepdims=False)
    visible = (key_pos[None, :] <= query_pos[:, None])[None, None]

    q4 = queries.reshape(tok_rows, kv_local, group, head_size)
    do4 = cotangent.reshape(tok_rows, kv_local, group, head_size)
    scores = jnp.einsum("qgjd,kgd->gjqk", q4, key_heads, preferred_element_type=jnp.float32) * scale
    scores = jnp.where(visible, scores, NEG)
    top_score = jnp.max(scores, axis=-1, keepdims=True)
    totals = jnp.sum(jnp.where(visible, jnp.exp(scores - top_score), 0.0), axis=-1, keepdims=True)
    log_total = top_score + jnp.log(totals)
    probs = jnp.where(visible, jnp.exp(scores - log_total), 0.0)
    probs_low = probs.astype(jnp.bfloat16)
    attended = jnp.einsum(
        "gjqk,kgd->qgjd", probs_low, value_heads, preferred_element_type=jnp.float32
    )
    delta = jnp.sum(do4.astype(jnp.float32) * attended, axis=-1)
    dprobs = jnp.einsum("qgjd,kgd->gjqk", do4, value_heads, preferred_element_type=jnp.float32)
    dscores = (probs * (dprobs - jnp.transpose(delta, (1, 2, 0))[..., None])).astype(jnp.bfloat16)
    q_grad = (
        jnp.einsum("gjqk,kgd->qgjd", dscores, key_heads, preferred_element_type=jnp.float32) * scale
    ).astype(jnp.bfloat16)
    key_grad = jnp.einsum("gjqk,qgjd->kgd", dscores, q4, preferred_element_type=jnp.float32) * scale
    value_grad = jnp.einsum("gjqk,qgjd->kgd", probs_low, do4, preferred_element_type=jnp.float32)

    attended_flat = attended.astype(jnp.bfloat16).reshape(tok_rows, heads_local * head_size)
    q_grad_flat = q_grad.reshape(tok_rows, heads_local * head_size)
    grad_terms = jnp.stack([key_grad, value_grad], axis=2).reshape(seq_rows, 2 * kv_width)
    grad_parts = lax.all_to_all(
        grad_terms.astype(jnp.bfloat16), plane, split_axis=0, concat_axis=0, tiled=True
    )
    grad_parts = grad_parts.reshape(ctx_count, tp_count, kv_rows, kv_local, 2, head_size)
    own_grads = jnp.sum(grad_parts.astype(jnp.float32), axis=0)
    k_grad_tokens = own_grads[:, :, :, 0, :].transpose(1, 0, 2, 3).reshape(kv_rows, -1)
    v_grad_tokens = own_grads[:, :, :, 1, :].transpose(1, 0, 2, 3).reshape(kv_rows, -1)
    return (attended_flat[None], q_grad_flat[None], k_grad_tokens[None], v_grad_tokens[None])


def solution(mesh):
    in_specs = (
        P(),
        P(),
        P("section", None, "ctx", "tp"),
        P("section", None, ("ctx", "tp"), None),
        P("section", None, ("ctx", "tp"), None),
        P("section", "ctx", "tp"),
    )
    out_specs = (
        P("section", "ctx", "tp"),
        P("section", "ctx", "tp"),
        P("section", ("ctx", "tp"), None),
        P("section", ("ctx", "tp"), None),
    )
    return jax.shard_map(plane_step, mesh=mesh, in_specs=in_specs, out_specs=out_specs, check_vma=False)
```

```python
import functools

import jax
import jax.numpy as jnp
from jax import lax
from jax.sharding import PartitionSpec as P
from jax.experimental import pallas as pl
from jax.experimental.pallas import tpu as pltpu

HEAD_DIM = 128


NEG = -1e30


NT = (((1,), (1,)), ((), ()))


def head_kernel(scale, qpos_ref, kpos_ref, q_ref, do_ref, k_ref, v_ref, att_ref, dq_ref, dkv_ref, acc_ref):
    h = pl.program_id(0)
    width = k_ref.shape[1]

    @pl.when(h == 0)
    def _():
        acc_ref[...] = jnp.zeros_like(acc_ref)

    q = q_ref[...]
    do = do_ref[...]
    k = k_ref[...]
    v = v_ref[...]
    visible = kpos_ref[...] <= qpos_ref[...]
    scores = lax.dot_general(q, k, NT, preferred_element_type=jnp.float32) * scale
    scores = jnp.where(visible, scores, NEG)
    top = jnp.max(scores, axis=1, keepdims=True)
    totals = jnp.sum(jnp.where(visible, jnp.exp(scores - top), 0.0), axis=1, keepdims=True)
    log_total = top + jnp.log(totals)
    probs = jnp.where(visible, jnp.exp(scores - log_total), 0.0)
    probs_low = probs.astype(jnp.bfloat16)
    attended = jnp.dot(probs_low, v, preferred_element_type=jnp.float32)
    att_ref[...] = attended.astype(att_ref.dtype)
    delta = jnp.sum(do.astype(jnp.float32) * attended, axis=1, keepdims=True)
    dprobs = lax.dot_general(do, v, NT, preferred_element_type=jnp.float32)
    dscores_f = probs * (dprobs - delta)
    dscores = dscores_f.astype(jnp.bfloat16)
    dq = jnp.dot(dscores, k, preferred_element_type=jnp.float32) * scale
    dq_ref[...] = dq.astype(dq_ref.dtype)
    acc_ref[:, :width] += jnp.dot(
        dscores_f.T.astype(jnp.bfloat16), q, preferred_element_type=jnp.float32
    )
    acc_ref[:, width:] += jnp.dot(probs.T.astype(jnp.bfloat16), do, preferred_element_type=jnp.float32)

    @pl.when(h == pl.num_programs(0) - 1)
    def _():
        dkv_ref[:, :width] = (acc_ref[:, :width] * scale).astype(dkv_ref.dtype)
        dkv_ref[:, width:] = acc_ref[:, width:].astype(dkv_ref.dtype)


def head_attention(queries, cotangent, kv_full, query_pos, key_pos, head_size):
    rows, features = queries.shape
    seq = kv_full.shape[0]
    heads = features // head_size
    scale = head_size ** (-0.5)
    head_block = pl.BlockSpec((rows, head_size), lambda h: (0, h))
    flops = heads * 6 * 2 * rows * seq * head_size
    return pl.pallas_call(
        functools.partial(head_kernel, scale),
        grid=(heads,),
        in_specs=[
            pl.BlockSpec((rows, 1), lambda h: (0, 0)),
            pl.BlockSpec((1, seq), lambda h: (0, 0)),
            head_block,
            head_block,
            pl.BlockSpec((seq, head_size), lambda h: (0, 0)),
            pl.BlockSpec((seq, head_size), lambda h: (0, 1)),
        ],
        out_specs=[head_block, head_block, pl.BlockSpec((seq, 2 * head_size), lambda h: (0, 0))],
        out_shape=[
            jax.ShapeDtypeStruct((rows, features), jnp.bfloat16),
            jax.ShapeDtypeStruct((rows, features), jnp.bfloat16),
            jax.ShapeDtypeStruct((seq, 2 * head_size), jnp.bfloat16),
        ],
        scratch_shapes=[pltpu.VMEM((seq, 2 * head_size), jnp.float32)],
        compiler_params=pltpu.CompilerParams(dimension_semantics=("arbitrary",)),
        cost_estimate=pl.CostEstimate(
            flops=flops, transcendentals=2 * heads * rows * seq, bytes_accessed=4 * rows * features * 2 + seq * 2 * head_size * 4
        ),
    )(query_pos.reshape(rows, 1), key_pos.reshape(1, seq), queries, cotangent, kv_full, kv_full)


def passed_along(block, axis, distance):
    devices = range(lax.axis_size(axis))
    route = [((i - distance) % len(devices), i) for i in devices]
    return lax.ppermute(block, axis, route)


def body(block_order, plan, q_box, k_box, v_box, grad_out):
    tp_count = lax.axis_size("tp")
    ctx_count = lax.axis_size("ctx")
    section_count = lax.axis_size("section")
    tok_rows = q_box.shape[2]
    kv_rows = k_box.shape[2]
    seq_rows = tok_rows * ctx_count
    block_len = seq_rows // block_order.shape[0]
    head_size = HEAD_DIM
    heads_local = q_box.shape[3] // head_size
    kv_local = k_box.shape[3] // head_size // tp_count
    group = heads_local // kv_local
    kv_width = kv_local * head_size
    scale = head_size ** (-0.5)
    section_rank = lax.axis_index("section")

    receiver = (section_rank + 1) % section_count
    wanted = lax.dynamic_index_in_dim(plan, receiver, 0, keepdims=False)
    q_send = lax.dynamic_index_in_dim(q_box[0], wanted, 0, keepdims=False)
    k_send = lax.dynamic_index_in_dim(k_box[0], wanted, 0, keepdims=False)
    v_send = lax.dynamic_index_in_dim(v_box[0], wanted, 0, keepdims=False)
    kv_send = jnp.stack(
        [k_send.reshape(kv_rows, -1, head_size), v_send.reshape(kv_rows, -1, head_size)], axis=2
    ).reshape(kv_rows, -1)
    queries, kv_rows_in = passed_along((q_send, kv_send), "section", 1)
    cotangent = passed_along(grad_out[0], "section", -1)

    plane = ("ctx", "tp")
    kv_pieces = kv_rows_in.reshape(1, kv_rows, tp_count, 2 * kv_width).transpose(0, 2, 1, 3)
    kv_pieces = jnp.broadcast_to(kv_pieces, (ctx_count, tp_count, kv_rows, 2 * kv_width))
    kv_pieces = kv_pieces.reshape(ctx_count * tp_count * kv_rows, 2 * kv_width)
    kv_full = lax.all_to_all(kv_pieces, plane, split_axis=0, concat_axis=0, tiled=True)
    ctx_rank = lax.axis_index("ctx")

    positions = (
        block_order[:, None] * block_len + jnp.arange(block_len, dtype=jnp.int32)[None, :]
    ).reshape(ctx_count, tok_rows)
    key_pos = positions.reshape(seq_rows)
    query_pos = lax.dynamic_index_in_dim(positions, ctx_rank, 0, keepdims=False)
    attended_flat, q_grad_flat, grad_terms = head_attention(
        queries, cotangent, kv_full.reshape(seq_rows, 2 * kv_width), query_pos, key_pos, head_size
    )

    grad_parts = lax.all_to_all(grad_terms, plane, split_axis=0, concat_axis=0, tiled=True)
    grad_parts = grad_parts.reshape(ctx_count, tp_count, kv_rows, kv_local, 2, head_size)
    own_grads = jnp.sum(grad_parts.astype(jnp.float32), axis=0)
    k_grad_tokens = own_grads[:, :, :, 0, :].transpose(1, 0, 2, 3).reshape(kv_rows, -1)
    v_grad_tokens = own_grads[:, :, :, 1, :].transpose(1, 0, 2, 3).reshape(kv_rows, -1)
    return (attended_flat[None], q_grad_flat[None], k_grad_tokens[None], v_grad_tokens[None])


def solution(mesh):
    in_specs = (
        P(),
        P(),
        P("section", None, "ctx", "tp"),
        P("section", None, ("ctx", "tp"), None),
        P("section", None, ("ctx", "tp"), None),
        P("section", "ctx", "tp"),
    )
    out_specs = (
        P("section", "ctx", "tp"),
        P("section", "ctx", "tp"),
        P("section", ("ctx", "tp"), None),
        P("section", ("ctx", "tp"), None),
    )
    return jax.shard_map(body, mesh=mesh, in_specs=in_specs, out_specs=out_specs, check_vma=False)
```

```python
import jax
import jax.numpy as jnp
from jax import lax
from jax.sharding import PartitionSpec as P

HEAD_DIM = 128


NEG = -1e30


def passed_along(block, axis, distance):
    devices = range(lax.axis_size(axis))
    route = [((i - distance) % len(devices), i) for i in devices]
    return lax.ppermute(block, axis, route)


def body(block_order, plan, q_box, k_box, v_box, grad_out):
    tp_count = lax.axis_size("tp")
    ctx_count = lax.axis_size("ctx")
    section_count = lax.axis_size("section")
    tok_rows = q_box.shape[2]
    kv_rows = k_box.shape[2]
    seq_rows = tok_rows * ctx_count
    block_len = seq_rows // block_order.shape[0]
    head_size = HEAD_DIM
    heads_local = q_box.shape[3] // head_size
    kv_local = k_box.shape[3] // head_size // tp_count
    group = heads_local // kv_local
    kv_width = kv_local * head_size
    scale = head_size ** (-0.5)
    section_rank = lax.axis_index("section")

    receiver = (section_rank + 1) % section_count
    wanted = lax.dynamic_index_in_dim(plan, receiver, 0, keepdims=False)
    q_send = lax.dynamic_index_in_dim(q_box[0], wanted, 0, keepdims=False)
    k_send = lax.dynamic_index_in_dim(k_box[0], wanted, 0, keepdims=False)
    v_send = lax.dynamic_index_in_dim(v_box[0], wanted, 0, keepdims=False)
    kv_send = jnp.stack(
        [k_send.reshape(kv_rows, -1, head_size), v_send.reshape(kv_rows, -1, head_size)], axis=2
    ).reshape(kv_rows, -1)
    queries, kv_rows_in = passed_along((q_send, kv_send), "section", 1)
    cotangent = passed_along(grad_out[0], "section", -1)

    plane = ("ctx", "tp")
    kv_pieces = kv_rows_in.reshape(1, kv_rows, tp_count, 2 * kv_width).transpose(0, 2, 1, 3)
    kv_pieces = jnp.broadcast_to(kv_pieces, (ctx_count, tp_count, kv_rows, 2 * kv_width))
    kv_pieces = kv_pieces.reshape(ctx_count * tp_count * kv_rows, 2 * kv_width)
    kv_full = lax.all_to_all(kv_pieces, plane, split_axis=0, concat_axis=0, tiled=True)
    kv_full = kv_full.reshape(seq_rows, kv_local, 2, head_size)
    key_heads = kv_full[:, :, 0, :]
    value_heads = kv_full[:, :, 1, :]
    ctx_rank = lax.axis_index("ctx")

    positions = (
        block_order[:, None] * block_len + jnp.arange(block_len, dtype=jnp.int32)[None, :]
    ).reshape(ctx_count, tok_rows)
    key_pos = positions.reshape(seq_rows)
    query_pos = lax.dynamic_index_in_dim(positions, ctx_rank, 0, keepdims=False)
    visible = (key_pos[None, :] <= query_pos[:, None])[None, None]

    q4 = queries.reshape(tok_rows, kv_local, group, head_size)
    do4 = cotangent.reshape(tok_rows, kv_local, group, head_size)
    scores = jnp.einsum("qgjd,kgd->gjqk", q4, key_heads, preferred_element_type=jnp.float32) * scale
    scores = jnp.where(visible, scores, NEG)
    top_score = jnp.max(scores, axis=-1, keepdims=True)
    shifted = jnp.exp(scores - top_score)
    totals = jnp.sum(shifted, axis=-1, keepdims=True)
    probs = shifted / totals
    probs_low = probs.astype(jnp.bfloat16)
    attended = jnp.einsum(
        "gjqk,kgd->qgjd", probs_low, value_heads, preferred_element_type=jnp.float32
    )
    delta = jnp.sum(do4.astype(jnp.float32) * attended, axis=-1)
    dprobs = jnp.einsum("qgjd,kgd->gjqk", do4, value_heads, preferred_element_type=jnp.float32)
    dscores = (probs * (dprobs - jnp.transpose(delta, (1, 2, 0))[..., None])).astype(jnp.bfloat16)
    q_grad = (
        jnp.einsum("gjqk,kgd->qgjd", dscores, key_heads, preferred_element_type=jnp.float32) * scale
    ).astype(jnp.bfloat16)
    key_grad = jnp.einsum("gjqk,qgjd->kgd", dscores, q4, preferred_element_type=jnp.float32) * scale
    value_grad = jnp.einsum("gjqk,qgjd->kgd", probs_low, do4, preferred_element_type=jnp.float32)

    attended_flat = attended.astype(jnp.bfloat16).reshape(tok_rows, heads_local * head_size)
    q_grad_flat = q_grad.reshape(tok_rows, heads_local * head_size)
    grad_terms = jnp.stack([key_grad, value_grad], axis=2).reshape(seq_rows, 2 * kv_width)
    grad_parts = lax.all_to_all(
        grad_terms.astype(jnp.bfloat16), plane, split_axis=0, concat_axis=1, tiled=True
    )
    grad_parts = grad_parts.reshape(kv_rows, ctx_count, tp_count * kv_local, 2, head_size)
    own_grads = jnp.sum(grad_parts.astype(jnp.float32), axis=1)
    k_grad_tokens = own_grads[:, :, 0, :].reshape(kv_rows, -1)
    v_grad_tokens = own_grads[:, :, 1, :].reshape(kv_rows, -1)
    return (attended_flat[None], q_grad_flat[None], k_grad_tokens[None], v_grad_tokens[None])


def solution(mesh):
    in_specs = (
        P(),
        P(),
        P("section", None, "ctx", "tp"),
        P("section", None, ("ctx", "tp"), None),
        P("section", None, ("ctx", "tp"), None),
        P("section", "ctx", "tp"),
    )
    out_specs = (
        P("section", "ctx", "tp"),
        P("section", "ctx", "tp"),
        P("section", ("ctx", "tp"), None),
        P("section", ("ctx", "tp"), None),
    )
    return jax.shard_map(body, mesh=mesh, in_specs=in_specs, out_specs=out_specs, check_vma=False)
```

```python
import jax
import jax.numpy as jnp
from jax import lax
from jax.sharding import PartitionSpec as P

HEAD_DIM = 128


NEG = -1e30


def passed_along(block, axis, distance):
    devices = range(lax.axis_size(axis))
    route = [((i - distance) % len(devices), i) for i in devices]
    return lax.ppermute(block, axis, route)


def body(block_order, plan, q_box, k_box, v_box, grad_out):
    tp_count = lax.axis_size("tp")
    ctx_count = lax.axis_size("ctx")
    section_count = lax.axis_size("section")
    tok_rows = q_box.shape[2]
    kv_rows = k_box.shape[2]
    seq_rows = tok_rows * ctx_count
    block_len = seq_rows // block_order.shape[0]
    head_size = HEAD_DIM
    heads_local = q_box.shape[3] // head_size
    kv_local = k_box.shape[3] // head_size // tp_count
    group = heads_local // kv_local
    kv_width = kv_local * head_size
    scale = head_size ** (-0.5)
    section_rank = lax.axis_index("section")

    receiver = (section_rank + 1) % section_count
    wanted = lax.dynamic_index_in_dim(plan, receiver, 0, keepdims=False)
    q_send = lax.dynamic_index_in_dim(q_box[0], wanted, 0, keepdims=False)
    k_send = lax.dynamic_index_in_dim(k_box[0], wanted, 0, keepdims=False)
    v_send = lax.dynamic_index_in_dim(v_box[0], wanted, 0, keepdims=False)
    kv_send = jnp.stack(
        [
            k_send.reshape(kv_rows, tp_count, kv_width).transpose(1, 0, 2),
            v_send.reshape(kv_rows, tp_count, kv_width).transpose(1, 0, 2),
        ],
        axis=1,
    ).reshape(tp_count, 2 * kv_rows, kv_width)
    queries, kv_rows_in = passed_along((q_send, kv_send), "section", 1)
    cotangent = passed_along(grad_out[0], "section", -1)

    plane = ("ctx", "tp")
    kv_pieces = jnp.broadcast_to(kv_rows_in[None], (ctx_count, tp_count, 2 * kv_rows, kv_width))
    kv_pieces = kv_pieces.reshape(ctx_count * tp_count * 2 * kv_rows, kv_width)
    kv_full = lax.all_to_all(kv_pieces, plane, split_axis=0, concat_axis=0, tiled=True)
    kv_full = kv_full.reshape(ctx_count * tp_count, 2, kv_rows, kv_local, head_size)
    key_heads = kv_full[:, 0].reshape(seq_rows, kv_local, head_size)
    value_heads = kv_full[:, 1].reshape(seq_rows, kv_local, head_size)
    ctx_rank = lax.axis_index("ctx")

    positions = (
        block_order[:, None] * block_len + jnp.arange(block_len, dtype=jnp.int32)[None, :]
    ).reshape(ctx_count, tok_rows)
    key_pos = positions.reshape(seq_rows)
    query_pos = lax.dynamic_index_in_dim(positions, ctx_rank, 0, keepdims=False)
    visible = (key_pos[None, :] <= query_pos[:, None])[None, None]

    q4 = queries.reshape(tok_rows, kv_local, group, head_size)
    do4 = cotangent.reshape(tok_rows, kv_local, group, head_size)
    scores = jnp.einsum("qgjd,kgd->gjqk", q4, key_heads, preferred_element_type=jnp.float32) * scale
    scores = jnp.where(visible, scores, NEG)
    top_score = jnp.max(scores, axis=-1, keepdims=True)
    shifted = jnp.exp(scores - top_score)
    totals = jnp.sum(shifted, axis=-1, keepdims=True)
    probs = shifted / totals
    probs_low = probs.astype(jnp.bfloat16)
    attended = jnp.einsum(
        "gjqk,kgd->qgjd", probs_low, value_heads, preferred_element_type=jnp.float32
    )
    delta = jnp.sum(do4.astype(jnp.float32) * attended, axis=-1)
    dprobs = jnp.einsum("qgjd,kgd->gjqk", do4, value_heads, preferred_element_type=jnp.float32)
    dscores = (probs * (dprobs - jnp.transpose(delta, (1, 2, 0))[..., None])).astype(jnp.bfloat16)
    q_grad = (
        jnp.einsum("gjqk,kgd->qgjd", dscores, key_heads, preferred_element_type=jnp.float32) * scale
    ).astype(jnp.bfloat16)
    key_grad = jnp.einsum("gjqk,qgjd->kgd", dscores, q4, preferred_element_type=jnp.float32) * scale
    value_grad = jnp.einsum("gjqk,qgjd->kgd", probs_low, do4, preferred_element_type=jnp.float32)

    attended_flat = attended.astype(jnp.bfloat16).reshape(tok_rows, heads_local * head_size)
    q_grad_flat = q_grad.reshape(tok_rows, heads_local * head_size)
    grad_terms = jnp.stack(
        [
            key_grad.reshape(ctx_count * tp_count, kv_rows, kv_width),
            value_grad.reshape(ctx_count * tp_count, kv_rows, kv_width),
        ],
        axis=1,
    ).reshape(seq_rows * 2, kv_width)
    grad_parts = lax.all_to_all(
        grad_terms.astype(jnp.bfloat16), plane, split_axis=0, concat_axis=0, tiled=True
    )
    grad_parts = grad_parts.reshape(ctx_count, tp_count, 2, kv_rows, kv_width)
    own_grads = jnp.sum(grad_parts.astype(jnp.float32), axis=0)
    k_grad_tokens = own_grads[:, 0].transpose(1, 0, 2).reshape(kv_rows, -1)
    v_grad_tokens = own_grads[:, 1].transpose(1, 0, 2).reshape(kv_rows, -1)
    return (attended_flat[None], q_grad_flat[None], k_grad_tokens[None], v_grad_tokens[None])


def solution(mesh):
    in_specs = (
        P(),
        P(),
        P("section", None, "ctx", "tp"),
        P("section", None, ("ctx", "tp"), None),
        P("section", None, ("ctx", "tp"), None),
        P("section", "ctx", "tp"),
    )
    out_specs = (
        P("section", "ctx", "tp"),
        P("section", "ctx", "tp"),
        P("section", ("ctx", "tp"), None),
        P("section", ("ctx", "tp"), None),
    )
    return jax.shard_map(body, mesh=mesh, in_specs=in_specs, out_specs=out_specs, check_vma=False)
```

```python
import jax
import jax.numpy as jnp
from jax import lax
from jax.sharding import PartitionSpec as P

HEAD_DIM = 128


NEG = -1e30


def passed_along(block, axis, distance):
    devices = range(lax.axis_size(axis))
    route = [((i - distance) % len(devices), i) for i in devices]
    return lax.ppermute(block, axis, route)


def body(block_order, plan, q_box, k_box, v_box, grad_out):
    tp_count = lax.axis_size("tp")
    ctx_count = lax.axis_size("ctx")
    section_count = lax.axis_size("section")
    tok_rows = q_box.shape[2]
    kv_rows = k_box.shape[2]
    seq_rows = tok_rows * ctx_count
    block_len = seq_rows // block_order.shape[0]
    head_size = HEAD_DIM
    heads_local = q_box.shape[3] // head_size
    kv_local = k_box.shape[3] // head_size // tp_count
    group = heads_local // kv_local
    kv_width = kv_local * head_size
    scale = head_size ** (-0.5)
    section_rank = lax.axis_index("section")

    receiver = (section_rank + 1) % section_count
    wanted = lax.dynamic_index_in_dim(plan, receiver, 0, keepdims=False)
    q_send = lax.dynamic_index_in_dim(q_box[0], wanted, 0, keepdims=False)
    k_send = lax.dynamic_index_in_dim(k_box[0], wanted, 0, keepdims=False)
    v_send = lax.dynamic_index_in_dim(v_box[0], wanted, 0, keepdims=False)
    kv_send = jnp.stack(
        [k_send.reshape(kv_rows, -1, head_size), v_send.reshape(kv_rows, -1, head_size)], axis=2
    ).reshape(kv_rows, -1)
    queries, kv_rows_in = passed_along((q_send, kv_send), "section", 1)
    cotangent = passed_along(grad_out[0], "section", -1)

    plane = ("ctx", "tp")
    kv_pieces = kv_rows_in.reshape(1, kv_rows, tp_count, 2 * kv_width).transpose(0, 2, 1, 3)
    kv_pieces = jnp.broadcast_to(kv_pieces, (ctx_count, tp_count, kv_rows, 2 * kv_width))
    kv_pieces = kv_pieces.reshape(ctx_count * tp_count * kv_rows, 2 * kv_width)
    kv_full = lax.all_to_all(kv_pieces, plane, split_axis=0, concat_axis=0, tiled=True)
    kv_full = kv_full.reshape(seq_rows, kv_local, 2, head_size)
    key_heads = kv_full[:, :, 0, :]
    value_heads = kv_full[:, :, 1, :]
    ctx_rank = lax.axis_index("ctx")

    positions = (
        block_order[:, None] * block_len + jnp.arange(block_len, dtype=jnp.int32)[None, :]
    ).reshape(ctx_count, tok_rows)
    key_pos = positions.reshape(seq_rows)
    query_pos = lax.dynamic_index_in_dim(positions, ctx_rank, 0, keepdims=False)
    visible = (key_pos[None, :] <= query_pos[:, None])[None, None]

    q4 = queries.reshape(tok_rows, kv_local, group, head_size)
    do4 = cotangent.reshape(tok_rows, kv_local, group, head_size)
    scores = jnp.einsum("qgjd,kgd->gjqk", q4, key_heads, preferred_element_type=jnp.float32) * scale
    scores = jnp.where(visible, scores, NEG)
    top_score = jnp.max(scores, axis=-1, keepdims=True)
    totals = jnp.sum(jnp.where(visible, jnp.exp(scores - top_score), 0.0), axis=-1, keepdims=True)
    log_total = top_score + jnp.log(totals)
    probs = jnp.where(visible, jnp.exp(scores - log_total), 0.0)
    probs_low = probs.astype(jnp.bfloat16)
    attended = jnp.einsum(
        "gjqk,kgd->qgjd", probs_low, value_heads, preferred_element_type=jnp.float32
    )
    delta = jnp.sum(do4.astype(jnp.float32) * attended, axis=-1)
    dprobs = jnp.einsum("qgjd,kgd->gjqk", do4, value_heads, preferred_element_type=jnp.float32)
    dscores = (probs * (dprobs - jnp.transpose(delta, (1, 2, 0))[..., None])).astype(jnp.bfloat16)
    q_grad = (
        jnp.einsum("gjqk,kgd->qgjd", dscores, key_heads, preferred_element_type=jnp.float32) * scale
    ).astype(jnp.bfloat16)
    key_grad = jnp.einsum("gjqk,qgjd->kgd", dscores, q4, preferred_element_type=jnp.float32) * scale
    value_grad = jnp.einsum("gjqk,qgjd->kgd", probs_low, do4, preferred_element_type=jnp.float32)

    attended_flat = attended.astype(jnp.bfloat16).reshape(tok_rows, heads_local * head_size)
    q_grad_flat = q_grad.reshape(tok_rows, heads_local * head_size)
    grad_terms = jnp.stack([key_grad, value_grad], axis=2).reshape(seq_rows, 2 * kv_width)
    grad_parts = lax.all_to_all(
        grad_terms.astype(jnp.bfloat16), plane, split_axis=0, concat_axis=1, tiled=True
    )
    grad_parts = grad_parts.reshape(kv_rows, ctx_count, tp_count * kv_local, 2, head_size)
    own_grads = jnp.sum(grad_parts.astype(jnp.float32), axis=1)
    k_grad_tokens = own_grads[:, :, 0, :].reshape(kv_rows, -1)
    v_grad_tokens = own_grads[:, :, 1, :].reshape(kv_rows, -1)
    return (attended_flat[None], q_grad_flat[None], k_grad_tokens[None], v_grad_tokens[None])


def solution(mesh):
    in_specs = (
        P(),
        P(),
        P("section", None, "ctx", "tp"),
        P("section", None, ("ctx", "tp"), None),
        P("section", None, ("ctx", "tp"), None),
        P("section", "ctx", "tp"),
    )
    out_specs = (
        P("section", "ctx", "tp"),
        P("section", "ctx", "tp"),
        P("section", ("ctx", "tp"), None),
        P("section", ("ctx", "tp"), None),
    )
    return jax.shard_map(body, mesh=mesh, in_specs=in_specs, out_specs=out_specs, check_vma=False)
```

```python
import jax
import jax.numpy as jnp
from jax import lax
from jax.sharding import PartitionSpec as P

HEAD_DIM = 128


NEG = -1e30


def passed_along(block, axis, distance):
    devices = range(lax.axis_size(axis))
    route = [((i - distance) % len(devices), i) for i in devices]
    return lax.ppermute(block, axis, route)


def body(block_order, plan, q_box, k_box, v_box, grad_out):
    tp_count = lax.axis_size("tp")
    ctx_count = lax.axis_size("ctx")
    section_count = lax.axis_size("section")
    tok_rows = q_box.shape[2]
    kv_rows = k_box.shape[2]
    seq_rows = tok_rows * ctx_count
    block_len = seq_rows // block_order.shape[0]
    head_size = HEAD_DIM
    heads_local = q_box.shape[3] // head_size
    kv_local = k_box.shape[3] // head_size // tp_count
    group = heads_local // kv_local
    kv_width = kv_local * head_size
    scale = head_size ** (-0.5)
    section_rank = lax.axis_index("section")

    receiver = (section_rank + 1) % section_count
    wanted = lax.dynamic_index_in_dim(plan, receiver, 0, keepdims=False)
    def pick(box):
        slots = box[0]
        chosen = slots[0]
        for slot in range(1, slots.shape[0]):
            chosen = jnp.where(wanted == slot, slots[slot], chosen)
        return chosen

    q_send = pick(q_box)
    k_send = pick(k_box)
    v_send = pick(v_box)
    kv_send = jnp.stack(
        [k_send.reshape(kv_rows, -1, head_size), v_send.reshape(kv_rows, -1, head_size)], axis=2
    ).reshape(kv_rows, -1)
    queries, kv_rows_in = passed_along((q_send, kv_send), "section", 1)
    cotangent = passed_along(grad_out[0], "section", -1)

    plane = ("ctx", "tp")
    kv_pieces = kv_rows_in.reshape(1, kv_rows, tp_count, 2 * kv_width).transpose(0, 2, 1, 3)
    kv_pieces = jnp.broadcast_to(kv_pieces, (ctx_count, tp_count, kv_rows, 2 * kv_width))
    kv_pieces = kv_pieces.reshape(ctx_count * tp_count * kv_rows, 2 * kv_width)
    kv_full = lax.all_to_all(kv_pieces, plane, split_axis=0, concat_axis=0, tiled=True)
    kv_full = kv_full.reshape(seq_rows, kv_local, 2, head_size)
    key_heads = kv_full[:, :, 0, :]
    value_heads = kv_full[:, :, 1, :]
    ctx_rank = lax.axis_index("ctx")

    positions = (
        block_order[:, None] * block_len + jnp.arange(block_len, dtype=jnp.int32)[None, :]
    ).reshape(ctx_count, tok_rows)
    key_pos = positions.reshape(seq_rows)
    query_pos = lax.dynamic_index_in_dim(positions, ctx_rank, 0, keepdims=False)
    visible = (key_pos[None, :] <= query_pos[:, None])[None, None]

    q4 = queries.reshape(tok_rows, kv_local, group, head_size)
    do4 = cotangent.reshape(tok_rows, kv_local, group, head_size)
    scores = jnp.einsum("qgjd,kgd->gjqk", q4, key_heads, preferred_element_type=jnp.float32) * scale
    scores = jnp.where(visible, scores, NEG)
    top_score = jnp.max(scores, axis=-1, keepdims=True)
    totals = jnp.sum(jnp.where(visible, jnp.exp(scores - top_score), 0.0), axis=-1, keepdims=True)
    log_total = top_score + jnp.log(totals)
    probs = jnp.where(visible, jnp.exp(scores - log_total), 0.0)
    probs_low = probs.astype(jnp.bfloat16)
    attended = jnp.einsum(
        "gjqk,kgd->qgjd", probs_low, value_heads, preferred_element_type=jnp.float32
    )
    delta = jnp.sum(do4.astype(jnp.float32) * attended, axis=-1)
    dprobs = jnp.einsum("qgjd,kgd->gjqk", do4, value_heads, preferred_element_type=jnp.float32)
    dscores = (probs * (dprobs - jnp.transpose(delta, (1, 2, 0))[..., None])).astype(jnp.bfloat16)
    q_grad = (
        jnp.einsum("gjqk,kgd->qgjd", dscores, key_heads, preferred_element_type=jnp.float32) * scale
    ).astype(jnp.bfloat16)
    key_grad = jnp.einsum("gjqk,qgjd->kgd", dscores, q4, preferred_element_type=jnp.float32) * scale
    value_grad = jnp.einsum("gjqk,qgjd->kgd", probs_low, do4, preferred_element_type=jnp.float32)

    attended_flat = attended.astype(jnp.bfloat16).reshape(tok_rows, heads_local * head_size)
    q_grad_flat = q_grad.reshape(tok_rows, heads_local * head_size)
    grad_terms = jnp.stack([key_grad, value_grad], axis=2).reshape(seq_rows, 2 * kv_width)
    grad_parts = lax.all_to_all(
        grad_terms.astype(jnp.bfloat16), plane, split_axis=0, concat_axis=1, tiled=True
    )
    grad_parts = grad_parts.reshape(kv_rows, ctx_count, tp_count * kv_local, 2, head_size)
    own_grads = jnp.sum(grad_parts.astype(jnp.float32), axis=1)
    k_grad_tokens = own_grads[:, :, 0, :].reshape(kv_rows, -1)
    v_grad_tokens = own_grads[:, :, 1, :].reshape(kv_rows, -1)
    return (attended_flat[None], q_grad_flat[None], k_grad_tokens[None], v_grad_tokens[None])


def solution(mesh):
    in_specs = (
        P(),
        P(),
        P("section", None, "ctx", "tp"),
        P("section", None, ("ctx", "tp"), None),
        P("section", None, ("ctx", "tp"), None),
        P("section", "ctx", "tp"),
    )
    out_specs = (
        P("section", "ctx", "tp"),
        P("section", "ctx", "tp"),
        P("section", ("ctx", "tp"), None),
        P("section", ("ctx", "tp"), None),
    )
    return jax.shard_map(body, mesh=mesh, in_specs=in_specs, out_specs=out_specs, check_vma=False)
```

```python
import jax
import jax.numpy as jnp
from jax import lax
from jax.sharding import PartitionSpec as P

HEAD_DIM = 128


NEG = -1e30


def passed_along(block, axis, distance):
    devices = range(lax.axis_size(axis))
    route = [((i - distance) % len(devices), i) for i in devices]
    return lax.ppermute(block, axis, route)


def body(block_order, plan, q_box, k_box, v_box, grad_out):
    tp_count = lax.axis_size("tp")
    ctx_count = lax.axis_size("ctx")
    section_count = lax.axis_size("section")
    tok_rows = q_box.shape[2]
    kv_rows = k_box.shape[2]
    seq_rows = tok_rows * ctx_count
    block_len = seq_rows // block_order.shape[0]
    head_size = HEAD_DIM
    heads_local = q_box.shape[3] // head_size
    kv_local = k_box.shape[3] // head_size // tp_count
    group = heads_local // kv_local
    kv_width = kv_local * head_size
    scale = head_size ** (-0.5)
    section_rank = lax.axis_index("section")

    receiver = (section_rank + 1) % section_count
    wanted = lax.dynamic_index_in_dim(plan, receiver, 0, keepdims=False)

    def pick(box):
        slots = box[0]
        chosen = slots[0]
        for slot in range(1, slots.shape[0]):
            chosen = jnp.where(wanted == slot, slots[slot], chosen)
        return chosen

    q_send = pick(q_box)
    slot_count = k_box.shape[1]
    kv_both = jnp.stack(
        [
            k_box[0].reshape(slot_count, kv_rows, -1, head_size),
            v_box[0].reshape(slot_count, kv_rows, -1, head_size),
        ],
        axis=3,
    ).reshape(slot_count, kv_rows, -1)
    queries, kv_both_in = passed_along((q_send, kv_both), "section", 1)
    own_wanted = lax.dynamic_index_in_dim(plan, section_rank, 0, keepdims=False)
    kv_rows_in = kv_both_in[0]
    for slot in range(1, slot_count):
        kv_rows_in = jnp.where(own_wanted == slot, kv_both_in[slot], kv_rows_in)
    cotangent = passed_along(grad_out[0], "section", -1)

    plane = ("ctx", "tp")
    kv_pieces = kv_rows_in.reshape(1, kv_rows, tp_count, 2 * kv_width).transpose(0, 2, 1, 3)
    kv_pieces = jnp.broadcast_to(kv_pieces, (ctx_count, tp_count, kv_rows, 2 * kv_width))
    kv_pieces = kv_pieces.reshape(ctx_count * tp_count * kv_rows, 2 * kv_width)
    kv_full = lax.all_to_all(kv_pieces, plane, split_axis=0, concat_axis=0, tiled=True)
    kv_full = kv_full.reshape(seq_rows, kv_local, 2, head_size)
    key_heads = kv_full[:, :, 0, :]
    value_heads = kv_full[:, :, 1, :]
    ctx_rank = lax.axis_index("ctx")

    positions = (
        block_order[:, None] * block_len + jnp.arange(block_len, dtype=jnp.int32)[None, :]
    ).reshape(ctx_count, tok_rows)
    key_pos = positions.reshape(seq_rows)
    query_pos = lax.dynamic_index_in_dim(positions, ctx_rank, 0, keepdims=False)
    visible = (key_pos[None, :] <= query_pos[:, None])[None, None]

    q4 = queries.reshape(tok_rows, kv_local, group, head_size)
    do4 = cotangent.reshape(tok_rows, kv_local, group, head_size)
    scores = jnp.einsum("qgjd,kgd->gjqk", q4, key_heads, preferred_element_type=jnp.float32) * scale
    scores = jnp.where(visible, scores, NEG)
    top_score = jnp.max(scores, axis=-1, keepdims=True)
    totals = jnp.sum(jnp.where(visible, jnp.exp(scores - top_score), 0.0), axis=-1, keepdims=True)
    log_total = top_score + jnp.log(totals)
    probs = jnp.where(visible, jnp.exp(scores - log_total), 0.0)
    probs_low = probs.astype(jnp.bfloat16)
    attended = jnp.einsum(
        "gjqk,kgd->qgjd", probs_low, value_heads, preferred_element_type=jnp.float32
    )
    delta = jnp.sum(do4.astype(jnp.float32) * attended, axis=-1)
    dprobs = jnp.einsum("qgjd,kgd->gjqk", do4, value_heads, preferred_element_type=jnp.float32)
    dscores = (probs * (dprobs - jnp.transpose(delta, (1, 2, 0))[..., None])).astype(jnp.bfloat16)
    q_grad = (
        jnp.einsum("gjqk,kgd->qgjd", dscores, key_heads, preferred_element_type=jnp.float32) * scale
    ).astype(jnp.bfloat16)
    key_grad = jnp.einsum("gjqk,qgjd->kgd", dscores, q4, preferred_element_type=jnp.float32) * scale
    value_grad = jnp.einsum("gjqk,qgjd->kgd", probs_low, do4, preferred_element_type=jnp.float32)

    attended_flat = attended.astype(jnp.bfloat16).reshape(tok_rows, heads_local * head_size)
    q_grad_flat = q_grad.reshape(tok_rows, heads_local * head_size)
    grad_terms = jnp.stack([key_grad, value_grad], axis=2).reshape(seq_rows, 2 * kv_width)
    grad_parts = lax.all_to_all(
        grad_terms.astype(jnp.bfloat16), plane, split_axis=0, concat_axis=1, tiled=True
    )
    grad_parts = grad_parts.reshape(kv_rows, ctx_count, tp_count * kv_local, 2, head_size)
    own_grads = jnp.sum(grad_parts.astype(jnp.float32), axis=1)
    k_grad_tokens = own_grads[:, :, 0, :].reshape(kv_rows, -1)
    v_grad_tokens = own_grads[:, :, 1, :].reshape(kv_rows, -1)
    return (attended_flat[None], q_grad_flat[None], k_grad_tokens[None], v_grad_tokens[None])


def solution(mesh):
    in_specs = (
        P(),
        P(),
        P("section", None, "ctx", "tp"),
        P("section", None, ("ctx", "tp"), None),
        P("section", None, ("ctx", "tp"), None),
        P("section", "ctx", "tp"),
    )
    out_specs = (
        P("section", "ctx", "tp"),
        P("section", "ctx", "tp"),
        P("section", ("ctx", "tp"), None),
        P("section", ("ctx", "tp"), None),
    )
    return jax.shard_map(body, mesh=mesh, in_specs=in_specs, out_specs=out_specs, check_vma=False)
```

```python
import jax
import jax.numpy as jnp
from jax import lax
from jax.sharding import PartitionSpec as P

HEAD_DIM = 128


NEG = -1e30


def passed_along(block, axis, distance):
    devices = range(lax.axis_size(axis))
    route = [((i - distance) % len(devices), i) for i in devices]
    return lax.ppermute(block, axis, route)


def body(block_order, plan, q_box, k_box, v_box, grad_out):
    tp_count = lax.axis_size("tp")
    ctx_count = lax.axis_size("ctx")
    section_count = lax.axis_size("section")
    tok_rows = q_box.shape[2]
    kv_rows = k_box.shape[2]
    seq_rows = tok_rows * ctx_count
    block_len = seq_rows // block_order.shape[0]
    head_size = HEAD_DIM
    heads_local = q_box.shape[3] // head_size
    kv_local = k_box.shape[3] // head_size // tp_count
    group = heads_local // kv_local
    kv_width = kv_local * head_size
    scale = head_size ** (-0.5)
    section_rank = lax.axis_index("section")

    receiver = (section_rank + 1) % section_count
    wanted = jnp.sum(jnp.where(jnp.arange(section_count) == receiver, plan, 0))

    def pick(box):
        slots = box[0]
        chosen = slots[0]
        for slot in range(1, slots.shape[0]):
            chosen = jnp.where(wanted == slot, slots[slot], chosen)
        return chosen

    q_send = pick(q_box)
    k_send = pick(k_box)
    v_send = pick(v_box)
    kv_send = jnp.stack(
        [k_send.reshape(kv_rows, -1, head_size), v_send.reshape(kv_rows, -1, head_size)], axis=2
    ).reshape(kv_rows, -1)
    queries, kv_rows_in = passed_along((q_send, kv_send), "section", 1)
    cotangent = passed_along(grad_out[0], "section", -1)

    plane = ("ctx", "tp")
    kv_pieces = kv_rows_in.reshape(1, kv_rows, tp_count, 2 * kv_width).transpose(0, 2, 1, 3)
    kv_pieces = jnp.broadcast_to(kv_pieces, (ctx_count, tp_count, kv_rows, 2 * kv_width))
    kv_pieces = kv_pieces.reshape(ctx_count * tp_count * kv_rows, 2 * kv_width)
    kv_full = lax.all_to_all(kv_pieces, plane, split_axis=0, concat_axis=0, tiled=True)
    kv_full = kv_full.reshape(seq_rows, kv_local, 2, head_size)
    key_heads = kv_full[:, :, 0, :]
    value_heads = kv_full[:, :, 1, :]
    ctx_rank = lax.axis_index("ctx")

    positions = (
        block_order[:, None] * block_len + jnp.arange(block_len, dtype=jnp.int32)[None, :]
    ).reshape(ctx_count, tok_rows)
    key_pos = positions.reshape(seq_rows)
    query_pos = lax.dynamic_index_in_dim(positions, ctx_rank, 0, keepdims=False)
    visible = (key_pos[None, :] <= query_pos[:, None])[None, None]

    q4 = queries.reshape(tok_rows, kv_local, group, head_size)
    do4 = cotangent.reshape(tok_rows, kv_local, group, head_size)
    scores = jnp.einsum("qgjd,kgd->gjqk", q4, key_heads, preferred_element_type=jnp.float32) * scale
    scores = jnp.where(visible, scores, NEG)
    top_score = jnp.max(scores, axis=-1, keepdims=True)
    totals = jnp.sum(jnp.where(visible, jnp.exp(scores - top_score), 0.0), axis=-1, keepdims=True)
    log_total = top_score + jnp.log(totals)
    probs = jnp.where(visible, jnp.exp(scores - log_total), 0.0)
    probs_low = probs.astype(jnp.bfloat16)
    attended = jnp.einsum(
        "gjqk,kgd->qgjd", probs_low, value_heads, preferred_element_type=jnp.float32
    )
    delta = jnp.sum(do4.astype(jnp.float32) * attended, axis=-1)
    dprobs = jnp.einsum("qgjd,kgd->gjqk", do4, value_heads, preferred_element_type=jnp.float32)
    dscores = (probs * (dprobs - jnp.transpose(delta, (1, 2, 0))[..., None])).astype(jnp.bfloat16)
    q_grad = (
        jnp.einsum("gjqk,kgd->qgjd", dscores, key_heads, preferred_element_type=jnp.float32) * scale
    ).astype(jnp.bfloat16)
    key_grad = jnp.einsum("gjqk,qgjd->kgd", dscores, q4, preferred_element_type=jnp.float32) * scale
    value_grad = jnp.einsum("gjqk,qgjd->kgd", probs_low, do4, preferred_element_type=jnp.float32)

    attended_flat = attended.astype(jnp.bfloat16).reshape(tok_rows, heads_local * head_size)
    q_grad_flat = q_grad.reshape(tok_rows, heads_local * head_size)
    grad_terms = jnp.stack([key_grad, value_grad], axis=2).reshape(seq_rows, 2 * kv_width)
    grad_parts = lax.all_to_all(
        grad_terms.astype(jnp.bfloat16), plane, split_axis=0, concat_axis=1, tiled=True
    )
    grad_parts = grad_parts.reshape(kv_rows, ctx_count, tp_count * kv_local, 2, head_size)
    own_grads = jnp.sum(grad_parts.astype(jnp.float32), axis=1)
    k_grad_tokens = own_grads[:, :, 0, :].reshape(kv_rows, -1)
    v_grad_tokens = own_grads[:, :, 1, :].reshape(kv_rows, -1)
    return (attended_flat[None], q_grad_flat[None], k_grad_tokens[None], v_grad_tokens[None])


def solution(mesh):
    in_specs = (
        P(),
        P(),
        P("section", None, "ctx", "tp"),
        P("section", None, ("ctx", "tp"), None),
        P("section", None, ("ctx", "tp"), None),
        P("section", "ctx", "tp"),
    )
    out_specs = (
        P("section", "ctx", "tp"),
        P("section", "ctx", "tp"),
        P("section", ("ctx", "tp"), None),
        P("section", ("ctx", "tp"), None),
    )
    return jax.shard_map(body, mesh=mesh, in_specs=in_specs, out_specs=out_specs, check_vma=False)
```

```python
import jax
import jax.numpy as jnp
from jax import lax
from jax.sharding import PartitionSpec as P

HEAD_DIM = 128


NEG = -1e30


def passed_along(block, axis, distance):
    devices = range(lax.axis_size(axis))
    route = [((i - distance) % len(devices), i) for i in devices]
    return lax.ppermute(block, axis, route)


def body(block_order, plan, q_box, k_box, v_box, grad_out):
    tp_count = lax.axis_size("tp")
    ctx_count = lax.axis_size("ctx")
    section_count = lax.axis_size("section")
    tok_rows = q_box.shape[2]
    kv_rows = k_box.shape[2]
    seq_rows = tok_rows * ctx_count
    block_len = seq_rows // block_order.shape[0]
    head_size = HEAD_DIM
    heads_local = q_box.shape[3] // head_size
    kv_local = k_box.shape[3] // head_size // tp_count
    group = heads_local // kv_local
    kv_width = kv_local * head_size
    scale = head_size ** (-0.5)
    section_rank = lax.axis_index("section")

    receiver = (section_rank + 1) % section_count
    wanted = lax.dynamic_index_in_dim(plan, receiver, 0, keepdims=False)
    def pick(box):
        slots = box[0]
        chosen = slots[0]
        for slot in range(1, slots.shape[0]):
            chosen = jnp.where(wanted == slot, slots[slot], chosen)
        return chosen

    q_send = pick(q_box)
    k_send = pick(k_box)
    v_send = pick(v_box)
    queries, k_in, v_in = passed_along((q_send, k_send, v_send), "section", 1)
    kv_rows_in = jnp.stack(
        [k_in.reshape(kv_rows, -1, head_size), v_in.reshape(kv_rows, -1, head_size)], axis=2
    ).reshape(kv_rows, -1)
    cotangent = passed_along(grad_out[0], "section", -1)

    plane = ("ctx", "tp")
    kv_pieces = kv_rows_in.reshape(1, kv_rows, tp_count, 2 * kv_width).transpose(0, 2, 1, 3)
    kv_pieces = jnp.broadcast_to(kv_pieces, (ctx_count, tp_count, kv_rows, 2 * kv_width))
    kv_pieces = kv_pieces.reshape(ctx_count * tp_count * kv_rows, 2 * kv_width)
    kv_full = lax.all_to_all(kv_pieces, plane, split_axis=0, concat_axis=0, tiled=True)
    kv_full = kv_full.reshape(seq_rows, kv_local, 2, head_size)
    key_heads = kv_full[:, :, 0, :]
    value_heads = kv_full[:, :, 1, :]
    ctx_rank = lax.axis_index("ctx")

    positions = (
        block_order[:, None] * block_len + jnp.arange(block_len, dtype=jnp.int32)[None, :]
    ).reshape(ctx_count, tok_rows)
    key_pos = positions.reshape(seq_rows)
    query_pos = lax.dynamic_index_in_dim(positions, ctx_rank, 0, keepdims=False)
    visible = (key_pos[None, :] <= query_pos[:, None])[None, None]

    q4 = queries.reshape(tok_rows, kv_local, group, head_size)
    do4 = cotangent.reshape(tok_rows, kv_local, group, head_size)
    scores = jnp.einsum("qgjd,kgd->gjqk", q4, key_heads, preferred_element_type=jnp.float32) * scale
    scores = jnp.where(visible, scores, NEG)
    top_score = jnp.max(scores, axis=-1, keepdims=True)
    totals = jnp.sum(jnp.where(visible, jnp.exp(scores - top_score), 0.0), axis=-1, keepdims=True)
    log_total = top_score + jnp.log(totals)
    probs = jnp.where(visible, jnp.exp(scores - log_total), 0.0)
    probs_low = probs.astype(jnp.bfloat16)
    attended = jnp.einsum(
        "gjqk,kgd->qgjd", probs_low, value_heads, preferred_element_type=jnp.float32
    )
    delta = jnp.sum(do4.astype(jnp.float32) * attended, axis=-1)
    dprobs = jnp.einsum("qgjd,kgd->gjqk", do4, value_heads, preferred_element_type=jnp.float32)
    dscores = (probs * (dprobs - jnp.transpose(delta, (1, 2, 0))[..., None])).astype(jnp.bfloat16)
    q_grad = (
        jnp.einsum("gjqk,kgd->qgjd", dscores, key_heads, preferred_element_type=jnp.float32) * scale
    ).astype(jnp.bfloat16)
    key_grad = jnp.einsum("gjqk,qgjd->kgd", dscores, q4, preferred_element_type=jnp.float32) * scale
    value_grad = jnp.einsum("gjqk,qgjd->kgd", probs_low, do4, preferred_element_type=jnp.float32)

    attended_flat = attended.astype(jnp.bfloat16).reshape(tok_rows, heads_local * head_size)
    q_grad_flat = q_grad.reshape(tok_rows, heads_local * head_size)
    grad_terms = jnp.stack([key_grad, value_grad], axis=2).reshape(seq_rows, 2 * kv_width)
    grad_parts = lax.all_to_all(
        grad_terms.astype(jnp.bfloat16), plane, split_axis=0, concat_axis=1, tiled=True
    )
    grad_parts = grad_parts.reshape(kv_rows, ctx_count, tp_count * kv_local, 2, head_size)
    own_grads = jnp.sum(grad_parts.astype(jnp.float32), axis=1)
    k_grad_tokens = own_grads[:, :, 0, :].reshape(kv_rows, -1)
    v_grad_tokens = own_grads[:, :, 1, :].reshape(kv_rows, -1)
    return (attended_flat[None], q_grad_flat[None], k_grad_tokens[None], v_grad_tokens[None])


def solution(mesh):
    in_specs = (
        P(),
        P(),
        P("section", None, "ctx", "tp"),
        P("section", None, ("ctx", "tp"), None),
        P("section", None, ("ctx", "tp"), None),
        P("section", "ctx", "tp"),
    )
    out_specs = (
        P("section", "ctx", "tp"),
        P("section", "ctx", "tp"),
        P("section", ("ctx", "tp"), None),
        P("section", ("ctx", "tp"), None),
    )
    return jax.shard_map(body, mesh=mesh, in_specs=in_specs, out_specs=out_specs, check_vma=False)
```

```python
import jax
import jax.numpy as jnp
from jax import lax
from jax.sharding import PartitionSpec as P

HEAD_DIM = 128


NEG = -1e30


def passed_along(block, axis, distance):
    devices = range(lax.axis_size(axis))
    route = [((i - distance) % len(devices), i) for i in devices]
    return lax.ppermute(block, axis, route)


def body(block_order, plan, q_box, k_box, v_box, grad_out):
    tp_count = lax.axis_size("tp")
    ctx_count = lax.axis_size("ctx")
    section_count = lax.axis_size("section")
    tok_rows = q_box.shape[2]
    kv_rows = k_box.shape[2]
    seq_rows = tok_rows * ctx_count
    block_len = seq_rows // block_order.shape[0]
    head_size = HEAD_DIM
    heads_local = q_box.shape[3] // head_size
    kv_local = k_box.shape[3] // head_size // tp_count
    group = heads_local // kv_local
    kv_width = kv_local * head_size
    scale = head_size ** (-0.5)
    section_rank = lax.axis_index("section")

    receiver = (section_rank + 1) % section_count
    wanted = lax.dynamic_index_in_dim(plan, receiver, 0, keepdims=False)
    def pick(box):
        slots = box[0]
        chosen = slots[0]
        for slot in range(1, slots.shape[0]):
            chosen = jnp.where(wanted == slot, slots[slot], chosen)
        return chosen

    q_send = pick(q_box)
    k_send = pick(k_box)
    v_send = pick(v_box)
    kv_send = jnp.stack(
        [k_send.reshape(kv_rows, -1, head_size), v_send.reshape(kv_rows, -1, head_size)], axis=2
    ).reshape(kv_rows, -1)
    queries, kv_rows_in = passed_along((q_send, kv_send), "section", 1)
    cotangent = passed_along(grad_out[0], "section", -1)

    plane = ("ctx", "tp")
    kv_pieces = kv_rows_in.reshape(1, kv_rows, tp_count, 2 * kv_width).transpose(0, 2, 1, 3)
    kv_pieces = jnp.broadcast_to(kv_pieces, (ctx_count, tp_count, kv_rows, 2 * kv_width))
    kv_pieces = kv_pieces.reshape(ctx_count * tp_count * kv_rows, 2 * kv_width)
    kv_full = lax.all_to_all(kv_pieces, plane, split_axis=0, concat_axis=0, tiled=True)
    kv_full = kv_full.reshape(seq_rows, kv_local, 2, head_size)
    key_heads = kv_full[:, :, 0, :]
    value_heads = kv_full[:, :, 1, :]
    ctx_rank = lax.axis_index("ctx")

    positions = (
        block_order[:, None] * block_len + jnp.arange(block_len, dtype=jnp.int32)[None, :]
    ).reshape(ctx_count, tok_rows)
    key_pos = positions.reshape(seq_rows)
    query_pos = lax.dynamic_index_in_dim(positions, ctx_rank, 0, keepdims=False)
    visible = (key_pos[None, :] <= query_pos[:, None])[None, None]

    q4 = queries.reshape(tok_rows, kv_local, group, head_size)
    do4 = cotangent.reshape(tok_rows, kv_local, group, head_size)
    scores = jnp.einsum("qgjd,kgd->gjqk", q4, key_heads, preferred_element_type=jnp.float32) * scale
    scores = jnp.where(visible, scores, NEG)
    top_score = jnp.max(scores, axis=-1, keepdims=True)
    totals = jnp.sum(jnp.exp(scores - top_score), axis=-1, keepdims=True)
    log_total = top_score + jnp.log(totals)
    probs = jnp.exp(scores - log_total)
    probs_low = probs.astype(jnp.bfloat16)
    attended = jnp.einsum(
        "gjqk,kgd->qgjd", probs_low, value_heads, preferred_element_type=jnp.float32
    )
    delta = jnp.sum(do4.astype(jnp.float32) * attended, axis=-1)
    dprobs = jnp.einsum("qgjd,kgd->gjqk", do4, value_heads, preferred_element_type=jnp.float32)
    dscores = (probs * (dprobs - jnp.transpose(delta, (1, 2, 0))[..., None])).astype(jnp.bfloat16)
    q_grad = (
        jnp.einsum("gjqk,kgd->qgjd", dscores, key_heads, preferred_element_type=jnp.float32) * scale
    ).astype(jnp.bfloat16)
    key_grad = jnp.einsum("gjqk,qgjd->kgd", dscores, q4, preferred_element_type=jnp.float32) * scale
    value_grad = jnp.einsum("gjqk,qgjd->kgd", probs_low, do4, preferred_element_type=jnp.float32)

    attended_flat = attended.astype(jnp.bfloat16).reshape(tok_rows, heads_local * head_size)
    q_grad_flat = q_grad.reshape(tok_rows, heads_local * head_size)
    grad_terms = jnp.stack([key_grad, value_grad], axis=2).reshape(seq_rows, 2 * kv_width)
    grad_parts = lax.all_to_all(
        grad_terms.astype(jnp.bfloat16), plane, split_axis=0, concat_axis=1, tiled=True
    )
    grad_parts = grad_parts.reshape(kv_rows, ctx_count, tp_count * kv_local, 2, head_size)
    own_grads = jnp.sum(grad_parts.astype(jnp.float32), axis=1)
    k_grad_tokens = own_grads[:, :, 0, :].reshape(kv_rows, -1)
    v_grad_tokens = own_grads[:, :, 1, :].reshape(kv_rows, -1)
    return (attended_flat[None], q_grad_flat[None], k_grad_tokens[None], v_grad_tokens[None])


def solution(mesh):
    in_specs = (
        P(),
        P(),
        P("section", None, "ctx", "tp"),
        P("section", None, ("ctx", "tp"), None),
        P("section", None, ("ctx", "tp"), None),
        P("section", "ctx", "tp"),
    )
    out_specs = (
        P("section", "ctx", "tp"),
        P("section", "ctx", "tp"),
        P("section", ("ctx", "tp"), None),
        P("section", ("ctx", "tp"), None),
    )
    return jax.shard_map(body, mesh=mesh, in_specs=in_specs, out_specs=out_specs, check_vma=False)
```
